32 devices in a mesh: dp: 4 (over z), seq: 8 (over y, x, core).
Axes of the slice: x: 2, y: 2, z: 4, core: 2. Of those that a mesh axis runs over, the one named last changes fastest.
Arguments:
- queries: bfloat16 [8, 2048, 2048], P('dp', 'seq'), may hold values from -6 to 6
- d_context: bfloat16 [8, 2048, 2048], P('dp', 'seq'), may hold values from -12 to 12
- database: bfloat16 [1024, 128, 896], P(('dp', 'seq')), may hold values from -6 to 6
- key_weight: bfloat16 [896, 2048], replicated, may hold values from -0.1875 to 0.1875
- value_weight: bfloat16 [896, 2048], replicated, may hold values from -0.1875 to 0.1875
- neighbour_shard: int32 [4, 8, 8, 2], P('dp', 'seq'), may hold values from 0 to 3, all different within a row; in each aligned block of 8 rows (0 to 7, 8 to 15, ..., all dimensions but the last counted through in order) at most 8 rows name the same one
- neighbour_row: int32 [4, 8, 8, 2], P('dp', 'seq'), may hold values from 0 to 31
Outputs:
- context: bfloat16 [8, 2048, 2048], P('dp', 'seq')
- query_grad: bfloat16 [8, 2048, 2048], P('dp', 'seq')
- database_grad: float32 [1024, 128, 896], P(('dp', 'seq'))
- key_weight_grad: float32 [896, 2048], P(('dp', 'seq'))
- value_weight_grad: float32 [896, 2048], P(('dp', 'seq'))
The draws below stay inside these ranges and needn't reach their ends.
Inputs may be any that keep to these rules, and one draw needn't show every extreme that they name: `neighbour_shard`: among the 8 rows of one device (aligned blocks of the first three dimensions taken together), no shard is named more than 8 times, a bound that some block reaches; the 2 neighbours of one block name different shards.
All inputs are finite; a program needn't handle non-finite values.
Results may differ from the reference program's by a relative error of at most 0.015.
Values may be sent and summed in bfloat16 or wider, within the bound.
No kernel may reach another device: no remote copies, remote signals or barrier semaphores. Data moves between devices by JAX's collectives and lax.ppermute only.
A program may use at most 192 MiB of HBM per device.

```python
import math
import jax
import jax.numpy as jnp
import numpy as np
from jax import lax

HEADS = 16
HD = 128
ENC = 896
SPAN = 64
NB_LEN = 128
NBR = 2
LEN = 2048
SEQS_DP = 2
HW = 2048
BLOCKS_DEV = 8
CAP = 8
ROWS_DEV = 32
BATCH = 8
DB_ROWS = 1024
N_DP = 4
N_SEQ = 8


def with_ends(array, rng, smallest, high):
    longest = array.shape.index(max(array.shape))
    spots = []
    for shift in (0, 1):
        where = [jax.random.randint(jax.random.fold_in(rng, axis), (), 0, length) for axis, length in enumerate(array.shape)]
        where[longest] = (where[longest] + shift) % array.shape[longest]
        spots.append(tuple(where))
    return array.at[spots[0]].set(smallest).at[spots[1]].set(high)


def block_levels(stream_key, dims, shards, smallest, top_value):
    loudness = 1.0
    for dim, blocks in shards:
        draws = jax.random.uniform(jax.random.fold_in(jax.random.fold_in(stream_key, 6), dim), (blocks,), jnp.float32, smallest / len(shards), top_value / len(shards))
        loudness = loudness * jnp.repeat(jnp.exp(draws), dims[dim] // blocks).reshape((-1,) + (1,) * (len(dims) - 1 - dim))
    return loudness


def shared_out(key, own, number, rows, number_of, top, reach, slope):
    order = jax.random.permutation(key, number_of)
    heavy_load, usual = shares(number_of, rows * top, reach, slope, True), shares(number_of, rows * top, reach, slope, False)
    places = jnp.arange(number_of)

    def named(tallies, rotation):
        used = int((tallies > 0).sum())
        fixed = max(1, used // 4)
        shifted = fixed + (places - fixed + rotation * (used - fixed)) % max(1, number_of - fixed)
        return jnp.zeros((number_of,), jnp.int32).at[order[jnp.where(places < fixed, places, shifted)]].set(jnp.asarray(tallies, jnp.int32))

    tallies = jnp.where(number % 4 == 0, named(heavy_load, number // 4), named(usual, number - number // 4 - 1))
    mixed = jax.random.permutation(jax.random.fold_in(own, 3), number_of)
    source_of, taker = mixed[0:number_of // 2 * 2:2], mixed[1:number_of // 2 * 2:2]
    margin = jnp.minimum(tallies[source_of] - 1, reach - tallies[taker]) // 2
    margin = jnp.where((source_of == order[0]) | (taker == order[0]) | (tallies[taker] == 0), 0, jnp.maximum(margin, 0))
    shifted = jax.random.randint(jax.random.fold_in(own, 4), (number_of // 2,), 0, 1 << 20) % (margin + 1)
    tallies = tallies.at[source_of].add(-shifted).at[taker].add(shifted)
    members = jnp.searchsorted(jnp.cumsum(tallies), jnp.arange(rows * top), side="right").astype(jnp.int32)
    table = members.reshape(top, rows).T
    table = table[jax.random.permutation(jax.random.fold_in(own, 1), rows)]
    rotation = jax.random.randint(jax.random.fold_in(own, 2), (rows, 1), 0, top)
    return jnp.take_along_axis(table, (jnp.arange(top)[None, :] + rotation) % top, axis=1)


def shares(number_of, total, bound, slope, full):
    weights = [(1 << 20) // math.isqrt(rank ** slope) + 1 for rank in range(1, number_of + 1)]
    largest = bound if full else min(bound, max(-(-total // number_of), total * weights[0] // sum(weights)))
    least = 1 if total - largest >= number_of - 1 else 0
    given, spare = [largest] + [least] * (number_of - 1), total - largest - least * (number_of - 1)
    while spare > 0:
        free = [i for i in range(1, number_of) if given[i] < largest] or [i for i in range(1, number_of) if given[i] < bound]
        whole, remaining = sum([weights[i] for i in free]), spare
        for i in free:
            extra = min(bound - given[i], max(1, remaining * weights[i] // whole), spare)
            given[i] = given[i] + extra
            spare = spare - extra
    return np.array(given)


def normal_values(rng, extent, spread, limit, split=(), kind=jnp.bfloat16):
    factor_of = block_levels(rng, extent, split, -0.22, 0.18) if split else 1.0
    array = jax.random.normal(rng, extent, jnp.float32) * spread * factor_of
    return jnp.minimum(jnp.maximum(array, -limit), limit).astype(kind)


def setup_inputs(seed: int = 0) -> dict:
    streams_of = jax.random.split(jax.random.key(seed), 8)
    queries = normal_values(streams_of[0], (BATCH, LEN, HW), 1.0, 6.0, ((0, 4), (1, 8)))
    d_context = normal_values(streams_of[1], (BATCH, LEN, HW), 2.0, 12.0, ((0, 4), (1, 8)))
    database = normal_values(streams_of[2], (DB_ROWS, NB_LEN, ENC), 1.0, 6.0, ((0, 32),))
    key_weight = normal_values(streams_of[3], (ENC, HW), ENC ** -0.5, 0.1875)
    value_weight = normal_values(streams_of[4], (ENC, HW), ENC ** -0.5, 0.1875)
    neighbour_shard_keys = jax.random.split(jax.random.fold_in(streams_of[5], 1), N_DP * N_SEQ * BLOCKS_DEV // BLOCKS_DEV)
    neighbour_shard_turns = jax.random.permutation(jax.random.fold_in(streams_of[5], 3), N_DP * N_SEQ * BLOCKS_DEV // BLOCKS_DEV)
    neighbour_shard = jax.vmap(lambda own, number: shared_out(jax.random.fold_in(streams_of[5], 2), own, number, BLOCKS_DEV, N_DP, NBR, CAP, 2))(neighbour_shard_keys, neighbour_shard_turns).reshape((N_DP, N_SEQ, BLOCKS_DEV, NBR))
    neighbour_row = with_ends(jax.random.randint(streams_of[6], (N_DP, N_SEQ, BLOCKS_DEV, NBR), 0, ROWS_DEV), jax.random.fold_in(streams_of[6], 1), 0, ROWS_DEV - 1).astype(jnp.int32)
    return dict(queries=queries, d_context=d_context, database=database, key_weight=key_weight, value_weight=value_weight, neighbour_shard=neighbour_shard, neighbour_row=neighbour_row)


def attend(query_block, grad_block, near_rows, key_weight, value_weight):
    score_scale = HD ** -0.5
    key_rows = jnp.dot(near_rows, key_weight, preferred_element_type=jnp.float32).astype(jnp.bfloat16)
    value_rows = jnp.dot(near_rows, value_weight, preferred_element_type=jnp.float32).astype(jnp.bfloat16)
    query_heads = query_block.astype(jnp.float32).reshape(SPAN, HEADS, HD)
    grad_heads = grad_block.astype(jnp.float32).reshape(SPAN, HEADS, HD)
    key_heads = key_rows.astype(jnp.float32).reshape(NBR * NB_LEN, HEADS, HD)
    value_heads = value_rows.astype(jnp.float32).reshape(NBR * NB_LEN, HEADS, HD)
    scores = jnp.einsum('qhd,khd->hqk', query_heads, key_heads) * score_scale
    weights = jnp.exp(scores)
    weights = weights / jnp.sum(weights, axis=-1, keepdims=True)
    weight_half = weights.astype(jnp.bfloat16)
    context_block = jnp.einsum('hqk,khd->qhd', weight_half.astype(jnp.float32), value_heads)
    context_block = context_block.astype(jnp.bfloat16).reshape(SPAN, HW)
    prob_grads = jnp.einsum('qhd,khd->hqk', grad_heads, value_heads)
    row_delta = jnp.sum(weights * prob_grads, axis=-1, keepdims=True)
    score_grads = (score_scale * weights * (prob_grads - row_delta)).astype(jnp.bfloat16)
    query_part = jnp.einsum('hqk,khd->qhd', score_grads.astype(jnp.float32), key_heads)
    query_part = query_part.astype(jnp.bfloat16).reshape(SPAN, HW)
    key_grads = jnp.einsum('hqk,qhd->khd', score_grads.astype(jnp.float32), query_heads)
    key_grads = key_grads.astype(jnp.bfloat16).reshape(NBR * NB_LEN, HW)
    value_grads = jnp.einsum('hqk,qhd->khd', weight_half.astype(jnp.float32), grad_heads)
    value_grads = value_grads.astype(jnp.bfloat16).reshape(NBR * NB_LEN, HW)
    proj_grads = jnp.concatenate([key_grads, value_grads], axis=1)
    both_weights = jnp.concatenate([key_weight, value_weight], axis=1)
    near_grads = jnp.dot(proj_grads, both_weights.T, preferred_element_type=jnp.float32)
    weight_term = jnp.dot(near_rows.T, proj_grads, preferred_element_type=jnp.float32)
    return context_block, query_part, near_grads, weight_term


def reference(queries, d_context, database, key_weight, value_weight, neighbour_shard, neighbour_row):
    lag_rows = SPAN - 1
    block_total = LEN // SPAN
    per_seq = LEN // (SPAN * N_SEQ)
    seq_index = jnp.arange(N_SEQ, dtype=jnp.int32)[None, :, None, None]
    rows = (neighbour_shard * N_SEQ + seq_index) * ROWS_DEV + neighbour_row
    rows = rows.reshape(N_DP, N_SEQ, SEQS_DP, per_seq, NBR).transpose(0, 2, 1, 3, 4)
    rows = rows.reshape(BATCH * block_total, NBR).astype(jnp.int32)
    padding = jnp.zeros((BATCH, lag_rows, HW), jnp.bfloat16)
    shifted_q = jnp.concatenate([queries[:, lag_rows:], padding], axis=1).reshape(BATCH * block_total, SPAN, HW)
    shifted_g = jnp.concatenate([d_context[:, lag_rows:], padding], axis=1).reshape(BATCH * block_total, SPAN, HW)

    def scan_step(accumulated, inputs):
        query_block, grad_block, picked = inputs
        near_rows = jnp.take(database, picked, axis=0).reshape(NBR * NB_LEN, ENC)
        context_block, query_part, near_grads, weight_term = attend(query_block, grad_block, near_rows, key_weight, value_weight)
        return accumulated + weight_term, (context_block, query_part, near_grads)

    start_sum = jnp.zeros((ENC, 2 * HW), jnp.float32)
    accumulated, (context_all, query_all, near_all) = lax.scan(scan_step, start_sum, (shifted_q, shifted_g, rows))
    context_all = context_all.reshape(BATCH, LEN, HW)
    query_all = query_all.reshape(BATCH, LEN, HW)
    context = jnp.concatenate([padding, context_all[:, :LEN - lag_rows]], axis=1)
    query_grad = jnp.concatenate([padding, query_all[:, :LEN - lag_rows]], axis=1)
    database_grad = jnp.zeros((DB_ROWS, NB_LEN, ENC), jnp.float32)
    database_grad = database_grad.at[rows.reshape(-1)].add(near_all.reshape(BATCH * block_total * NBR, NB_LEN, ENC))
    return context, query_grad, database_grad, accumulated[:, :HW], accumulated[:, HW:]
```

```python
import jax
import jax.numpy as jnp
from jax import lax
from jax.sharding import PartitionSpec as P

HD = 128
ENC = 896
SPAN = 64
NB_LEN = 128


def shifted(array, axis, by):
    count = lax.axis_size(axis)
    pairs = [(i, i + by) for i in range(count) if 0 <= i + by < count]
    return lax.ppermute(array, axis, pairs)


def local(queries, d_context, database, key_weight, value_weight, neighbour_shard, neighbour_row):
    seq_count, seq_span, feat_width = queries.shape
    head_count = feat_width // HD
    lag_rows = SPAN - 1
    block_count = seq_count * seq_span // SPAN
    pick_count = neighbour_shard.shape[-1]
    ref_count = block_count * pick_count
    shard_count = lax.axis_size("dp")
    capacity = 2 * ref_count // shard_count
    slot_count = shard_count * capacity
    near_len = pick_count * NB_LEN
    target = neighbour_shard.reshape(ref_count)
    wanted = neighbour_row.reshape(ref_count)
    owners = (target[:, None] == jnp.arange(shard_count, dtype=jnp.int32)[None, :]).astype(
        jnp.int32
    )
    before = jnp.cumsum(owners, axis=0) - owners
    slot_rank = jnp.sum(before * owners, axis=1)
    slot_index = target * capacity + slot_rank
    placed = (slot_index[:, None] == jnp.arange(slot_count, dtype=jnp.int32)[None, :]).astype(
        jnp.int32
    )
    request = jnp.sum(placed * wanted[:, None], axis=0)
    arrived = lax.all_to_all(request, "dp", split_axis=0, concat_axis=0, tiled=True)
    outgoing = jnp.take(database, arrived, axis=0)
    incoming = lax.all_to_all(outgoing, "dp", split_axis=0, concat_axis=0, tiled=True)
    neighbours = jnp.take(incoming, slot_index, axis=0).reshape(ref_count * NB_LEN, ENC)
    key_rows = jnp.dot(neighbours, key_weight, preferred_element_type=jnp.float32).astype(
        jnp.bfloat16
    )
    value_rows = jnp.dot(neighbours, value_weight, preferred_element_type=jnp.float32).astype(
        jnp.bfloat16
    )
    key_heads = key_rows.reshape(block_count, near_len, head_count, HD)
    value_heads = value_rows.reshape(block_count, near_len, head_count, HD)
    head_rows, head_grads = shifted((queries[:, :lag_rows], d_context[:, :lag_rows]), "seq", -1)
    query_blocks = jnp.concatenate([queries[:, lag_rows:], head_rows], axis=1).reshape(
        block_count, SPAN, head_count, HD
    )
    grad_blocks = jnp.concatenate([d_context[:, lag_rows:], head_grads], axis=1).reshape(
        block_count, SPAN, head_count, HD
    )
    score_scale = HD ** (-0.5)
    scores = (
        jnp.einsum("cqhd,ckhd->chqk", query_blocks, key_heads, preferred_element_type=jnp.float32)
        * score_scale
    )
    weights = jnp.exp(scores)
    weights = weights / jnp.sum(weights, axis=-1, keepdims=True)
    weight_half = weights.astype(jnp.bfloat16)
    context_shift = jnp.einsum(
        "chqk,ckhd->cqhd", weight_half, value_heads, preferred_element_type=jnp.float32
    )
    context_shift = context_shift.astype(jnp.bfloat16).reshape(seq_count, seq_span, feat_width)
    prob_grads = jnp.einsum(
        "cqhd,ckhd->chqk", grad_blocks, value_heads, preferred_element_type=jnp.float32
    )
    row_delta = jnp.sum(weights * prob_grads, axis=-1, keepdims=True)
    score_grads = (score_scale * weights * (prob_grads - row_delta)).astype(jnp.bfloat16)
    query_shift = jnp.einsum(
        "chqk,ckhd->cqhd", score_grads, key_heads, preferred_element_type=jnp.float32
    )
    query_shift = query_shift.astype(jnp.bfloat16).reshape(seq_count, seq_span, feat_width)
    key_grads = jnp.einsum(
        "chqk,cqhd->ckhd", score_grads, query_blocks, preferred_element_type=jnp.float32
    )
    key_grads = key_grads.astype(jnp.bfloat16).reshape(ref_count * NB_LEN, feat_width)
    value_grads = jnp.einsum(
        "chqk,cqhd->ckhd", weight_half, grad_blocks, preferred_element_type=jnp.float32
    )
    value_grads = value_grads.astype(jnp.bfloat16).reshape(ref_count * NB_LEN, feat_width)
    proj_grads = jnp.concatenate([key_grads, value_grads], axis=1)
    both_weights = jnp.concatenate([key_weight, value_weight], axis=1)
    near_grads = jnp.einsum(
        "pz,xz->px", proj_grads, both_weights, preferred_element_type=jnp.float32
    )
    near_grads = near_grads.reshape(ref_count, NB_LEN * ENC)
    slot_grads = jnp.einsum(
        "rs,rx->sx", placed.astype(jnp.float32), near_grads, precision=lax.Precision.HIGHEST
    )
    returned = lax.all_to_all(
        slot_grads.reshape(slot_count, NB_LEN, ENC).astype(jnp.bfloat16),
        "dp",
        split_axis=0,
        concat_axis=0,
        tiled=True,
    ).astype(jnp.float32)
    row_hits = (jnp.arange(database.shape[0], dtype=jnp.int32)[:, None] == arrived[None, :]).astype(
        jnp.float32
    )
    database_grad = jnp.einsum(
        "rs,sx->rx",
        row_hits,
        returned.reshape(slot_count, NB_LEN * ENC),
        precision=lax.Precision.HIGHEST,
    )
    database_grad = database_grad.reshape(database.shape)
    keep_rows = seq_span - lag_rows
    prior_context, prior_grads = shifted(
        (context_shift[:, keep_rows:], query_shift[:, keep_rows:]), "seq", 1
    )
    context = jnp.concatenate([prior_context, context_shift[:, :keep_rows]], axis=1)
    query_grad = jnp.concatenate([prior_grads, query_shift[:, :keep_rows]], axis=1)
    seq_total = lax.axis_size("seq")
    enc_share = ENC // (shard_count * seq_total)
    seq_major = (
        neighbours.reshape(ref_count * NB_LEN, shard_count, seq_total, enc_share)
        .transpose(0, 2, 1, 3)
        .reshape(ref_count * NB_LEN, ENC)
    )
    weight_terms = jnp.einsum(
        "px,pz->xz", seq_major, proj_grads, preferred_element_type=jnp.float32
    ).reshape(seq_total, shard_count * enc_share, 2 * feat_width)
    plane_sums = lax.psum_scatter(weight_terms, "seq", scatter_dimension=0, tiled=True)
    owned_grads = lax.psum_scatter(
        plane_sums.reshape(shard_count, enc_share, 2 * feat_width),
        "dp",
        scatter_dimension=0,
        tiled=True,
    ).reshape(enc_share, 2 * feat_width)
    return (
        context,
        query_grad,
        database_grad,
        owned_grads[:, :feat_width],
        owned_grads[:, feat_width:],
    )


def solution(mesh):
    return jax.shard_map(
        local,
        mesh=mesh,
        in_specs=(
            P("dp", "seq", None),
            P("dp", "seq", None),
            P(("dp", "seq"), None, None),
            P(),
            P(),
            P("dp", "seq", None, None),
            P("dp", "seq", None, None),
        ),
        out_specs=(
            P("dp", "seq", None),
            P("dp", "seq", None),
            P(("dp", "seq"), None, None),
            P(("dp", "seq"), None),
            P(("dp", "seq"), None),
        ),
        check_vma=False,
    )
```

```python
import jax
import jax.numpy as jnp
from jax import lax
from jax.sharding import PartitionSpec as P

HD = 128
ENC = 896
SPAN = 64
NB_LEN = 128
CHUNKS = 4


def shifted(array, axis, by):
    count = lax.axis_size(axis)
    pairs = [(i, i + by) for i in range(count) if 0 <= i + by < count]
    return lax.ppermute(array, axis, pairs)


def one_hot(index, count):
    return (index[:, None] == jnp.arange(count, dtype=jnp.int32)[None, :]).astype(jnp.int32)


def attend_chunk(query_blocks, grad_blocks, neighbours, key_weight, value_weight, head_count):
    block_count = query_blocks.shape[0]
    near_len = neighbours.shape[0] // block_count
    key_rows = jnp.dot(neighbours, key_weight, preferred_element_type=jnp.float32).astype(
        jnp.bfloat16
    )
    value_rows = jnp.dot(neighbours, value_weight, preferred_element_type=jnp.float32).astype(
        jnp.bfloat16
    )
    key_heads = key_rows.reshape(block_count, near_len, head_count, HD)
    value_heads = value_rows.reshape(block_count, near_len, head_count, HD)
    score_scale = HD ** (-0.5)
    scores = (
        jnp.einsum("cqhd,ckhd->chqk", query_blocks, key_heads, preferred_element_type=jnp.float32)
        * score_scale
    )
    weights = jnp.exp(scores)
    weights = weights / jnp.sum(weights, axis=-1, keepdims=True)
    weight_half = weights.astype(jnp.bfloat16)
    context_shift = jnp.einsum(
        "chqk,ckhd->cqhd", weight_half, value_heads, preferred_element_type=jnp.float32
    ).astype(jnp.bfloat16)
    prob_grads = jnp.einsum(
        "cqhd,ckhd->chqk", grad_blocks, value_heads, preferred_element_type=jnp.float32
    )
    row_delta = jnp.sum(weights * prob_grads, axis=-1, keepdims=True)
    score_grads = (score_scale * weights * (prob_grads - row_delta)).astype(jnp.bfloat16)
    query_shift = jnp.einsum(
        "chqk,ckhd->cqhd", score_grads, key_heads, preferred_element_type=jnp.float32
    ).astype(jnp.bfloat16)
    key_grads = jnp.einsum(
        "chqk,cqhd->ckhd", score_grads, query_blocks, preferred_element_type=jnp.float32
    ).astype(jnp.bfloat16)
    value_grads = jnp.einsum(
        "chqk,cqhd->ckhd", weight_half, grad_blocks, preferred_element_type=jnp.float32
    ).astype(jnp.bfloat16)
    feat_width = head_count * HD
    proj_grads = jnp.concatenate(
        [
            key_grads.reshape(block_count * near_len, feat_width),
            value_grads.reshape(block_count * near_len, feat_width),
        ],
        axis=1,
    )
    both_weights = jnp.concatenate([key_weight, value_weight], axis=1)
    near_grads = jnp.einsum(
        "pz,xz->px", proj_grads, both_weights, preferred_element_type=jnp.float32
    )
    return context_shift, query_shift, proj_grads, near_grads


def local(queries, d_context, database, key_weight, value_weight, neighbour_shard, neighbour_row):
    seq_count, seq_span, feat_width = queries.shape
    head_count = feat_width // HD
    lag_rows = SPAN - 1
    block_count = seq_count * seq_span // SPAN
    pick_count = neighbour_shard.shape[-1]
    ref_count = block_count * pick_count
    shard_count = lax.axis_size("dp")
    seq_total = lax.axis_size("seq")
    capacity = 2 * ref_count // shard_count
    chunk_count = CHUNKS if block_count % CHUNKS == 0 else 1
    chunk_blocks = block_count // chunk_count
    chunk_refs = chunk_blocks * pick_count
    chunk_cap = min(chunk_blocks, capacity)
    chunk_slots = shard_count * chunk_cap

    own = lax.axis_index("dp")
    target = neighbour_shard.reshape(chunk_count, chunk_refs)
    wanted = neighbour_row.reshape(chunk_count, chunk_refs)
    slot_indices = []
    requests = []
    slot_refs = []
    for g in range(chunk_count):
        owners = one_hot(target[g], shard_count)
        before = jnp.cumsum(owners, axis=0) - owners
        slot_rank = jnp.sum(before * owners, axis=1)
        asked = one_hot(target[g] * chunk_cap + slot_rank, chunk_slots)
        requests.append(
            jnp.sum(asked * wanted[g][:, None], axis=0).reshape(shard_count, 1, chunk_cap)
        )
        slot_index = ((own - target[g]) % shard_count) * chunk_cap + slot_rank
        placed = one_hot(slot_index, chunk_slots)
        ref_ids = jnp.arange(1, chunk_refs + 1, dtype=jnp.int32)
        slot_refs.append(jnp.sum(placed * ref_ids[:, None], axis=0))
        slot_indices.append(slot_index)
    request = jnp.concatenate(requests, axis=1)
    arrived = lax.all_to_all(request, "dp", split_axis=0, concat_axis=0, tiled=True)
    offsets = jnp.arange(shard_count, dtype=jnp.int32)
    sent_rows = jnp.take(arrived, (own + offsets) % shard_count, axis=0)

    def exchange(parts, direction):
        received = [parts[0]]
        for k in range(1, shard_count):
            pairs = [(i, (i + direction * k) % shard_count) for i in range(shard_count)]
            received.append(lax.ppermute(parts[k], "dp", pairs))
        return jnp.stack(received, axis=0)

    head_rows, head_grads = shifted((queries[:, :lag_rows], d_context[:, :lag_rows]), "seq", -1)
    query_blocks = jnp.concatenate([queries[:, lag_rows:], head_rows], axis=1).reshape(
        block_count, SPAN, head_count, HD
    )
    grad_blocks = jnp.concatenate([d_context[:, lag_rows:], head_grads], axis=1).reshape(
        block_count, SPAN, head_count, HD
    )

    enc_share = ENC // (shard_count * seq_total)
    context_parts = []
    query_parts = []
    returned_parts = []
    weight_terms = None
    for g in range(chunk_count):
        outgoing = jnp.take(database, sent_rows[:, g, :].reshape(chunk_slots), axis=0)
        incoming = exchange(outgoing.reshape(shard_count, chunk_cap, NB_LEN, ENC), 1)
        neighbours = jnp.take(
            incoming.reshape(chunk_slots, NB_LEN, ENC), slot_indices[g], axis=0
        ).reshape(chunk_refs * NB_LEN, ENC)
        blocks = slice(g * chunk_blocks, (g + 1) * chunk_blocks)
        context_shift, query_shift, proj_grads, near_grads = attend_chunk(
            query_blocks[blocks], grad_blocks[blocks], neighbours, key_weight, value_weight,
            head_count,
        )
        context_parts.append(context_shift)
        query_parts.append(query_shift)
        padded = jnp.concatenate(
            [
                jnp.zeros((1, NB_LEN, ENC), jnp.bfloat16),
                near_grads.astype(jnp.bfloat16).reshape(chunk_refs, NB_LEN, ENC),
            ],
            axis=0,
        )
        slot_grads = jnp.take(padded, slot_refs[g], axis=0)
        returned_parts.append(
            exchange(slot_grads.reshape(shard_count, chunk_cap, NB_LEN, ENC), -1)
        )
        seq_major = (
            neighbours.reshape(chunk_refs * NB_LEN, shard_count, seq_total, enc_share)
            .transpose(0, 2, 1, 3)
            .reshape(chunk_refs * NB_LEN, ENC)
        )
        term = jnp.einsum("px,pz->xz", seq_major, proj_grads, preferred_element_type=jnp.float32)
        weight_terms = term if weight_terms is None else weight_terms + term

    returned = jnp.stack(
        [part.reshape(shard_count, chunk_cap, NB_LEN * ENC) for part in returned_parts], axis=1
    ).reshape(shard_count * chunk_count * chunk_cap, NB_LEN * ENC)
    row_hits = one_hot(sent_rows.reshape(-1), database.shape[0]).astype(jnp.bfloat16)
    database_grad = jnp.einsum(
        "sr,sx->rx", row_hits, returned, preferred_element_type=jnp.float32
    ).reshape(database.shape)

    context_shift = jnp.concatenate(context_parts, axis=0).reshape(seq_count, seq_span, feat_width)
    query_shift = jnp.concatenate(query_parts, axis=0).reshape(seq_count, seq_span, feat_width)
    keep_rows = seq_span - lag_rows
    prior_context, prior_grads = shifted(
        (context_shift[:, keep_rows:], query_shift[:, keep_rows:]), "seq", 1
    )
    context = jnp.concatenate([prior_context, context_shift[:, :keep_rows]], axis=1)
    query_grad = jnp.concatenate([prior_grads, query_shift[:, :keep_rows]], axis=1)

    plane_sums = lax.psum_scatter(
        weight_terms.reshape(seq_total, shard_count * enc_share, 2 * feat_width),
        "seq",
        scatter_dimension=0,
        tiled=True,
    )
    owned_grads = lax.psum_scatter(
        plane_sums.reshape(shard_count, enc_share, 2 * feat_width),
        "dp",
        scatter_dimension=0,
        tiled=True,
    ).reshape(enc_share, 2 * feat_width)
    return (
        context,
        query_grad,
        database_grad,
        owned_grads[:, :feat_width],
        owned_grads[:, feat_width:],
    )


def solution(mesh):
    return jax.shard_map(
        local,
        mesh=mesh,
        in_specs=(
            P("dp", "seq", None),
            P("dp", "seq", None),
            P(("dp", "seq"), None, None),
            P(),
            P(),
            P("dp", "seq", None, None),
            P("dp", "seq", None, None),
        ),
        out_specs=(
            P("dp", "seq", None),
            P("dp", "seq", None),
            P(("dp", "seq"), None, None),
            P(("dp", "seq"), None),
            P(("dp", "seq"), None),
        ),
        check_vma=False,
    )
```

```python
import jax
import jax.numpy as jnp
from jax import lax
from jax.sharding import PartitionSpec as P

HD = 128
ENC = 896
SPAN = 64
NB_LEN = 128
CHUNKS = 4
LEAD = 2


def shifted(array, axis, by):
    count = lax.axis_size(axis)
    pairs = [(i, i + by) for i in range(count) if 0 <= i + by < count]
    return lax.ppermute(array, axis, pairs)


def one_hot(index, count):
    return (index[:, None] == jnp.arange(count, dtype=jnp.int32)[None, :]).astype(jnp.int32)


def attend_chunk(query_blocks, grad_blocks, neighbours, key_weight, value_weight, head_count):
    block_count = query_blocks.shape[0]
    near_len = neighbours.shape[0] // block_count
    key_rows = jnp.dot(neighbours, key_weight, preferred_element_type=jnp.float32).astype(
        jnp.bfloat16
    )
    value_rows = jnp.dot(neighbours, value_weight, preferred_element_type=jnp.float32).astype(
        jnp.bfloat16
    )
    key_heads = key_rows.reshape(block_count, near_len, head_count, HD)
    value_heads = value_rows.reshape(block_count, near_len, head_count, HD)
    score_scale = HD ** (-0.5)
    scores = (
        jnp.einsum("cqhd,ckhd->chqk", query_blocks, key_heads, preferred_element_type=jnp.float32)
        * score_scale
    )
    weights = jnp.exp(scores)
    weights = weights / jnp.sum(weights, axis=-1, keepdims=True)
    weight_half = weights.astype(jnp.bfloat16)
    context_shift = jnp.einsum(
        "chqk,ckhd->cqhd", weight_half, value_heads, preferred_element_type=jnp.float32
    ).astype(jnp.bfloat16)
    prob_grads = jnp.einsum(
        "cqhd,ckhd->chqk", grad_blocks, value_heads, preferred_element_type=jnp.float32
    )
    row_delta = jnp.sum(weights * prob_grads, axis=-1, keepdims=True)
    score_grads = (score_scale * weights * (prob_grads - row_delta)).astype(jnp.bfloat16)
    query_shift = jnp.einsum(
        "chqk,ckhd->cqhd", score_grads, key_heads, preferred_element_type=jnp.float32
    ).astype(jnp.bfloat16)
    key_grads = jnp.einsum(
        "chqk,cqhd->ckhd", score_grads, query_blocks, preferred_element_type=jnp.float32
    ).astype(jnp.bfloat16)
    value_grads = jnp.einsum(
        "chqk,cqhd->ckhd", weight_half, grad_blocks, preferred_element_type=jnp.float32
    ).astype(jnp.bfloat16)
    feat_width = head_count * HD
    proj_grads = jnp.concatenate(
        [
            key_grads.reshape(block_count * near_len, feat_width),
            value_grads.reshape(block_count * near_len, feat_width),
        ],
        axis=1,
    )
    both_weights = jnp.concatenate([key_weight, value_weight], axis=1)
    near_grads = jnp.einsum(
        "pz,xz->px", proj_grads, both_weights, preferred_element_type=jnp.float32
    )
    return context_shift, query_shift, proj_grads, near_grads


def local(queries, d_context, database, key_weight, value_weight, neighbour_shard, neighbour_row):
    seq_count, seq_span, feat_width = queries.shape
    head_count = feat_width // HD
    lag_rows = SPAN - 1
    block_count = seq_count * seq_span // SPAN
    pick_count = neighbour_shard.shape[-1]
    ref_count = block_count * pick_count
    shard_count = lax.axis_size("dp")
    seq_total = lax.axis_size("seq")
    capacity = 2 * ref_count // shard_count
    chunk_count = CHUNKS if block_count % CHUNKS == 0 else 1
    chunk_blocks = block_count // chunk_count
    chunk_refs = chunk_blocks * pick_count
    chunk_cap = min(chunk_blocks, capacity)
    chunk_slots = shard_count * chunk_cap

    target = neighbour_shard.reshape(chunk_count, chunk_refs)
    wanted = neighbour_row.reshape(chunk_count, chunk_refs)
    slot_indices = []
    requests = []
    slot_refs = []
    for g in range(chunk_count):
        owners = one_hot(target[g], shard_count)
        before = jnp.cumsum(owners, axis=0) - owners
        slot_rank = jnp.sum(before * owners, axis=1)
        slot_index = target[g] * chunk_cap + slot_rank
        placed = one_hot(slot_index, chunk_slots)
        requests.append(
            jnp.sum(placed * wanted[g][:, None], axis=0).reshape(shard_count, 1, chunk_cap)
        )
        ref_ids = jnp.arange(1, chunk_refs + 1, dtype=jnp.int32)
        slot_refs.append(jnp.sum(placed * ref_ids[:, None], axis=0))
        slot_indices.append(slot_index)
    request = jnp.concatenate(requests, axis=1)
    arrived = lax.all_to_all(request, "dp", split_axis=0, concat_axis=0, tiled=True)

    head_rows, head_grads = shifted((queries[:, :lag_rows], d_context[:, :lag_rows]), "seq", -1)
    query_blocks = jnp.concatenate([queries[:, lag_rows:], head_rows], axis=1).reshape(
        block_count, SPAN, head_count, HD
    )
    grad_blocks = jnp.concatenate([d_context[:, lag_rows:], head_grads], axis=1).reshape(
        block_count, SPAN, head_count, HD
    )

    enc_share = ENC // (shard_count * seq_total)
    context_parts = []
    query_parts = []
    returned_parts = []
    markers = []
    seq_major = []
    proj_parts = []
    for g in range(chunk_count):
        outgoing = jnp.take(database, arrived[:, g, :].reshape(chunk_slots), axis=0)
        if g >= LEAD:
            outgoing, _ = lax.optimization_barrier((outgoing, markers[g - LEAD]))
        incoming = lax.all_to_all(outgoing, "dp", split_axis=0, concat_axis=0, tiled=True)
        neighbours = jnp.take(incoming, slot_indices[g], axis=0).reshape(
            chunk_refs * NB_LEN, ENC
        )
        blocks = slice(g * chunk_blocks, (g + 1) * chunk_blocks)
        context_shift, query_shift, proj_grads, near_grads = attend_chunk(
            query_blocks[blocks], grad_blocks[blocks], neighbours, key_weight, value_weight,
            head_count,
        )
        context_parts.append(context_shift)
        query_parts.append(query_shift)
        padded = jnp.concatenate(
            [
                jnp.zeros((1, NB_LEN, ENC), jnp.bfloat16),
                near_grads.astype(jnp.bfloat16).reshape(chunk_refs, NB_LEN, ENC),
            ],
            axis=0,
        )
        slot_grads = jnp.take(padded, slot_refs[g], axis=0)
        markers.append(slot_grads)
        returned_parts.append(
            lax.all_to_all(slot_grads, "dp", split_axis=0, concat_axis=0, tiled=True)
        )
        seq_major.append(
            neighbours.reshape(chunk_refs * NB_LEN, shard_count, seq_total, enc_share)
            .transpose(0, 2, 1, 3)
            .reshape(chunk_refs * NB_LEN, ENC)
        )
        proj_parts.append(proj_grads)

    def weight_term(first, last):
        return jnp.einsum(
            "px,pz->xz",
            jnp.concatenate(seq_major[first:last], axis=0),
            jnp.concatenate(proj_parts[first:last], axis=0),
            preferred_element_type=jnp.float32,
        )

    weight_terms = weight_term(chunk_count - 1, chunk_count)
    if chunk_count > 1:
        weight_terms = weight_term(0, chunk_count - 1) + weight_terms

    returned = jnp.stack(
        [part.reshape(shard_count, chunk_cap, NB_LEN * ENC) for part in returned_parts], axis=1
    ).reshape(shard_count * chunk_count * chunk_cap, NB_LEN * ENC)
    row_hits = one_hot(arrived.reshape(-1), database.shape[0]).astype(jnp.bfloat16)
    database_grad = jnp.einsum(
        "sr,sx->rx", row_hits, returned, preferred_element_type=jnp.float32
    ).reshape(database.shape)

    context_shift = jnp.concatenate(context_parts, axis=0).reshape(seq_count, seq_span, feat_width)
    query_shift = jnp.concatenate(query_parts, axis=0).reshape(seq_count, seq_span, feat_width)
    keep_rows = seq_span - lag_rows
    prior_context, prior_grads = shifted(
        (context_shift[:, keep_rows:], query_shift[:, keep_rows:]), "seq", 1
    )
    context = jnp.concatenate([prior_context, context_shift[:, :keep_rows]], axis=1)
    query_grad = jnp.concatenate([prior_grads, query_shift[:, :keep_rows]], axis=1)

    plane_sums = lax.psum_scatter(
        weight_terms.reshape(seq_total, shard_count * enc_share, 2 * feat_width),
        "seq",
        scatter_dimension=0,
        tiled=True,
    )
    owned_grads = lax.psum_scatter(
        plane_sums.reshape(shard_count, enc_share, 2 * feat_width),
        "dp",
        scatter_dimension=0,
        tiled=True,
    ).reshape(enc_share, 2 * feat_width)
    return (
        context,
        query_grad,
        database_grad,
        owned_grads[:, :feat_width],
        owned_grads[:, feat_width:],
    )


def solution(mesh):
    return jax.shard_map(
        local,
        mesh=mesh,
        in_specs=(
            P("dp", "seq", None),
            P("dp", "seq", None),
            P(("dp", "seq"), None, None),
            P(),
            P(),
            P("dp", "seq", None, None),
            P("dp", "seq", None, None),
        ),
        out_specs=(
            P("dp", "seq", None),
            P("dp", "seq", None),
            P(("dp", "seq"), None, None),
            P(("dp", "seq"), None),
            P(("dp", "seq"), None),
        ),
        check_vma=False,
    )
```

```python
import jax
import jax.numpy as jnp
from jax import lax
from jax.sharding import PartitionSpec as P

HD = 128
ENC = 896
SPAN = 64
NB_LEN = 128
CHUNKS = 4
LEAD = 2


def shifted(array, axis, by):
    count = lax.axis_size(axis)
    pairs = [(i, i + by) for i in range(count) if 0 <= i + by < count]
    return lax.ppermute(array, axis, pairs)


def one_hot(index, count):
    return (index[:, None] == jnp.arange(count, dtype=jnp.int32)[None, :]).astype(jnp.int32)


def attend_chunk(query_blocks, grad_blocks, neighbours, key_weight, value_weight, head_count):
    block_count = query_blocks.shape[0]
    near_len = neighbours.shape[0] // block_count
    key_rows = jnp.dot(neighbours, key_weight, preferred_element_type=jnp.float32).astype(
        jnp.bfloat16
    )
    value_rows = jnp.dot(neighbours, value_weight, preferred_element_type=jnp.float32).astype(
        jnp.bfloat16
    )
    key_heads = key_rows.reshape(block_count, near_len, head_count, HD)
    value_heads = value_rows.reshape(block_count, near_len, head_count, HD)
    score_scale = HD ** (-0.5)
    scores = (
        jnp.einsum("cqhd,ckhd->chqk", query_blocks, key_heads, preferred_element_type=jnp.float32)
        * score_scale
    )
    weights = jnp.exp(scores)
    weights = weights / jnp.sum(weights, axis=-1, keepdims=True)
    weight_half = weights.astype(jnp.bfloat16)
    context_shift = jnp.einsum(
        "chqk,ckhd->cqhd", weight_half, value_heads, preferred_element_type=jnp.float32
    ).astype(jnp.bfloat16)
    prob_grads = jnp.einsum(
        "cqhd,ckhd->chqk", grad_blocks, value_heads, preferred_element_type=jnp.float32
    )
    row_delta = jnp.sum(weights * prob_grads, axis=-1, keepdims=True)
    score_grads = (score_scale * weights * (prob_grads - row_delta)).astype(jnp.bfloat16)
    query_shift = jnp.einsum(
        "chqk,ckhd->cqhd", score_grads, key_heads, preferred_element_type=jnp.float32
    ).astype(jnp.bfloat16)
    key_grads = jnp.einsum(
        "chqk,cqhd->ckhd", score_grads, query_blocks, preferred_element_type=jnp.float32
    ).astype(jnp.bfloat16)
    value_grads = jnp.einsum(
        "chqk,cqhd->ckhd", weight_half, grad_blocks, preferred_element_type=jnp.float32
    ).astype(jnp.bfloat16)
    feat_width = head_count * HD
    proj_grads = jnp.concatenate(
        [
            key_grads.reshape(block_count * near_len, feat_width),
            value_grads.reshape(block_count * near_len, feat_width),
        ],
        axis=1,
    )
    both_weights = jnp.concatenate([key_weight, value_weight], axis=1)
    near_grads = jnp.einsum(
        "pz,xz->px", proj_grads, both_weights, preferred_element_type=jnp.float32
    )
    return context_shift, query_shift, proj_grads, near_grads


def local(queries, d_context, database, key_weight, value_weight, neighbour_shard, neighbour_row):
    seq_count, seq_span, feat_width = queries.shape
    head_count = feat_width // HD
    lag_rows = SPAN - 1
    block_count = seq_count * seq_span // SPAN
    pick_count = neighbour_shard.shape[-1]
    ref_count = block_count * pick_count
    shard_count = lax.axis_size("dp")
    seq_total = lax.axis_size("seq")
    capacity = 2 * ref_count // shard_count
    chunk_count = CHUNKS if block_count % CHUNKS == 0 else 1
    chunk_blocks = block_count // chunk_count
    chunk_refs = chunk_blocks * pick_count
    chunk_cap = min(chunk_blocks, capacity)
    chunk_slots = shard_count * chunk_cap

    target = neighbour_shard.reshape(chunk_count, chunk_refs)
    wanted = neighbour_row.reshape(chunk_count, chunk_refs)
    slot_indices = []
    requests = []
    slot_refs = []
    for g in range(chunk_count):
        owners = one_hot(target[g], shard_count)
        before = jnp.cumsum(owners, axis=0) - owners
        slot_rank = jnp.sum(before * owners, axis=1)
        slot_index = target[g] * chunk_cap + slot_rank
        placed = one_hot(slot_index, chunk_slots)
        requests.append(
            jnp.sum(placed * wanted[g][:, None], axis=0).reshape(shard_count, 1, chunk_cap)
        )
        ref_ids = jnp.arange(1, chunk_refs + 1, dtype=jnp.int32)
        slot_refs.append(jnp.sum(placed * ref_ids[:, None], axis=0))
        slot_indices.append(slot_index)
    request = jnp.concatenate(requests, axis=1)
    arrived = lax.all_to_all(request, "dp", split_axis=0, concat_axis=0, tiled=True)

    head_rows, head_grads = shifted((queries[:, :lag_rows], d_context[:, :lag_rows]), "seq", -1)
    query_blocks = jnp.concatenate([queries[:, lag_rows:], head_rows], axis=1).reshape(
        block_count, SPAN, head_count, HD
    )
    grad_blocks = jnp.concatenate([d_context[:, lag_rows:], head_grads], axis=1).reshape(
        block_count, SPAN, head_count, HD
    )

    enc_share = ENC // (shard_count * seq_total)
    context_parts = []
    query_parts = []
    database_grad = None
    markers = []
    seq_major = []
    proj_parts = []
    for g in range(chunk_count):
        outgoing = jnp.take(database, arrived[:, g, :].reshape(chunk_slots), axis=0)
        if g >= LEAD:
            outgoing, _ = lax.optimization_barrier((outgoing, markers[g - LEAD]))
        incoming = lax.all_to_all(outgoing, "dp", split_axis=0, concat_axis=0, tiled=True)
        neighbours = jnp.take(incoming, slot_indices[g], axis=0).reshape(
            chunk_refs * NB_LEN, ENC
        )
        blocks = slice(g * chunk_blocks, (g + 1) * chunk_blocks)
        context_shift, query_shift, proj_grads, near_grads = attend_chunk(
            query_blocks[blocks], grad_blocks[blocks], neighbours, key_weight, value_weight,
            head_count,
        )
        context_parts.append(context_shift)
        query_parts.append(query_shift)
        padded = jnp.concatenate(
            [
                jnp.zeros((1, NB_LEN, ENC), jnp.bfloat16),
                near_grads.astype(jnp.bfloat16).reshape(chunk_refs, NB_LEN, ENC),
            ],
            axis=0,
        )
        slot_grads = jnp.take(padded, slot_refs[g], axis=0)
        returned = lax.all_to_all(slot_grads, "dp", split_axis=0, concat_axis=0, tiled=True)
        markers.append(returned)
        row_hits = one_hot(arrived[:, g, :].reshape(chunk_slots), database.shape[0])
        part = jnp.einsum(
            "sr,sax->rax",
            row_hits.astype(jnp.bfloat16),
            returned,
            preferred_element_type=jnp.float32,
        )
        database_grad = part if database_grad is None else database_grad + part
        seq_major.append(
            neighbours.reshape(chunk_refs * NB_LEN, shard_count, seq_total, enc_share)
            .transpose(0, 2, 1, 3)
            .reshape(chunk_refs * NB_LEN, ENC)
        )
        proj_parts.append(proj_grads)

    def weight_term(first, last):
        return jnp.einsum(
            "px,pz->xz",
            jnp.concatenate(seq_major[first:last], axis=0),
            jnp.concatenate(proj_parts[first:last], axis=0),
            preferred_element_type=jnp.float32,
        )

    weight_terms = weight_term(chunk_count - 1, chunk_count)
    if chunk_count > 1:
        weight_terms = weight_term(0, chunk_count - 1) + weight_terms


    context_shift = jnp.concatenate(context_parts, axis=0).reshape(seq_count, seq_span, feat_width)
    query_shift = jnp.concatenate(query_parts, axis=0).reshape(seq_count, seq_span, feat_width)
    keep_rows = seq_span - lag_rows
    prior_context, prior_grads = shifted(
        (context_shift[:, keep_rows:], query_shift[:, keep_rows:]), "seq", 1
    )
    context = jnp.concatenate([prior_context, context_shift[:, :keep_rows]], axis=1)
    query_grad = jnp.concatenate([prior_grads, query_shift[:, :keep_rows]], axis=1)

    plane_sums = lax.psum_scatter(
        weight_terms.reshape(seq_total, shard_count * enc_share, 2 * feat_width),
        "seq",
        scatter_dimension=0,
        tiled=True,
    )
    owned_grads = lax.psum_scatter(
        plane_sums.reshape(shard_count, enc_share, 2 * feat_width),
        "dp",
        scatter_dimension=0,
        tiled=True,
    ).reshape(enc_share, 2 * feat_width)
    return (
        context,
        query_grad,
        database_grad,
        owned_grads[:, :feat_width],
        owned_grads[:, feat_width:],
    )


def solution(mesh):
    return jax.shard_map(
        local,
        mesh=mesh,
        in_specs=(
            P("dp", "seq", None),
            P("dp", "seq", None),
            P(("dp", "seq"), None, None),
            P(),
            P(),
            P("dp", "seq", None, None),
            P("dp", "seq", None, None),
        ),
        out_specs=(
            P("dp", "seq", None),
            P("dp", "seq", None),
            P(("dp", "seq"), None, None),
            P(("dp", "seq"), None),
            P(("dp", "seq"), None),
        ),
        check_vma=False,
    )
```

```python
import jax
import jax.numpy as jnp
from jax import lax
from jax.sharding import PartitionSpec as P

HD = 128
ENC = 896
SPAN = 64
NB_LEN = 128
CHUNKS = 4
LEAD = 2


def shifted(array, axis, by):
    count = lax.axis_size(axis)
    pairs = [(i, i + by) for i in range(count) if 0 <= i + by < count]
    return lax.ppermute(array, axis, pairs)


def one_hot(index, count):
    return (index[:, None] == jnp.arange(count, dtype=jnp.int32)[None, :]).astype(jnp.int32)


def attend_chunk(query_blocks, grad_blocks, neighbours, key_weight, value_weight, head_count):
    block_count = query_blocks.shape[0]
    near_len = neighbours.shape[0] // block_count
    key_rows = jnp.dot(neighbours, key_weight, preferred_element_type=jnp.float32).astype(
        jnp.bfloat16
    )
    value_rows = jnp.dot(neighbours, value_weight, preferred_element_type=jnp.float32).astype(
        jnp.bfloat16
    )
    key_heads = key_rows.reshape(block_count, near_len, head_count, HD)
    value_heads = value_rows.reshape(block_count, near_len, head_count, HD)
    score_scale = HD ** (-0.5)
    scores = (
        jnp.einsum("cqhd,ckhd->chqk", query_blocks, key_heads, preferred_element_type=jnp.float32)
        * score_scale
    )
    weights = jnp.exp(scores)
    weights = weights / jnp.sum(weights, axis=-1, keepdims=True)
    weight_half = weights.astype(jnp.bfloat16)
    context_shift = jnp.einsum(
        "chqk,ckhd->cqhd", weight_half, value_heads, preferred_element_type=jnp.float32
    ).astype(jnp.bfloat16)
    prob_grads = jnp.einsum(
        "cqhd,ckhd->chqk", grad_blocks, value_heads, preferred_element_type=jnp.float32
    )
    row_delta = jnp.sum(weights * prob_grads, axis=-1, keepdims=True)
    score_grads = (score_scale * weights * (prob_grads - row_delta)).astype(jnp.bfloat16)
    query_shift = jnp.einsum(
        "chqk,ckhd->cqhd", score_grads, key_heads, preferred_element_type=jnp.float32
    ).astype(jnp.bfloat16)
    key_grads = jnp.einsum(
        "chqk,cqhd->ckhd", score_grads, query_blocks, preferred_element_type=jnp.float32
    ).astype(jnp.bfloat16)
    value_grads = jnp.einsum(
        "chqk,cqhd->ckhd", weight_half, grad_blocks, preferred_element_type=jnp.float32
    ).astype(jnp.bfloat16)
    feat_width = head_count * HD
    proj_grads = jnp.concatenate(
        [
            key_grads.reshape(block_count * near_len, feat_width),
            value_grads.reshape(block_count * near_len, feat_width),
        ],
        axis=1,
    )
    both_weights = jnp.concatenate([key_weight, value_weight], axis=1)
    near_grads = jnp.einsum(
        "pz,xz->px", proj_grads, both_weights, preferred_element_type=jnp.float32
    )
    return context_shift, query_shift, proj_grads, near_grads


def local(queries, d_context, database, key_weight, value_weight, neighbour_shard, neighbour_row):
    seq_count, seq_span, feat_width = queries.shape
    head_count = feat_width // HD
    lag_rows = SPAN - 1
    block_count = seq_count * seq_span // SPAN
    pick_count = neighbour_shard.shape[-1]
    ref_count = block_count * pick_count
    shard_count = lax.axis_size("dp")
    seq_total = lax.axis_size("seq")
    capacity = 2 * ref_count // shard_count
    chunk_count = CHUNKS if block_count % CHUNKS == 0 else 1
    chunk_blocks = block_count // chunk_count
    chunk_refs = chunk_blocks * pick_count
    chunk_cap = min(chunk_blocks, capacity)
    chunk_slots = shard_count * chunk_cap

    target = neighbour_shard.reshape(chunk_count, chunk_refs)
    wanted = neighbour_row.reshape(chunk_count, chunk_refs)
    slot_indices = []
    requests = []
    slot_refs = []
    for g in range(chunk_count):
        owners = one_hot(target[g], shard_count)
        before = jnp.cumsum(owners, axis=0) - owners
        slot_rank = jnp.sum(before * owners, axis=1)
        slot_index = target[g] * chunk_cap + slot_rank
        placed = one_hot(slot_index, chunk_slots)
        requests.append(
            jnp.sum(placed * wanted[g][:, None], axis=0).reshape(shard_count, 1, chunk_cap)
        )
        ref_ids = jnp.arange(1, chunk_refs + 1, dtype=jnp.int32)
        slot_refs.append(jnp.sum(placed * ref_ids[:, None], axis=0))
        slot_indices.append(slot_index)
    request = jnp.concatenate(requests, axis=1)
    arrived = lax.all_to_all(request, "dp", split_axis=0, concat_axis=0, tiled=True)

    head_rows, head_grads = shifted((queries[:, :lag_rows], d_context[:, :lag_rows]), "seq", -1)
    query_blocks = jnp.concatenate([queries[:, lag_rows:], head_rows], axis=1).reshape(
        block_count, SPAN, head_count, HD
    )
    grad_blocks = jnp.concatenate([d_context[:, lag_rows:], head_grads], axis=1).reshape(
        block_count, SPAN, head_count, HD
    )

    enc_share = ENC // (shard_count * seq_total)
    context_parts = []
    query_parts = []
    returned_parts = []
    neighbour_parts = []
    grads_out = []
    seq_major = []
    proj_parts = []
    for step in range(chunk_count + 2):
        payload = []
        if step < chunk_count:
            rows = jnp.take(database, arrived[:, step, :].reshape(chunk_slots), axis=0)
            payload.append(rows.reshape(shard_count, chunk_cap, NB_LEN, ENC))
        if step >= 2:
            payload.append(grads_out[step - 2].reshape(shard_count, chunk_cap, NB_LEN, ENC))
        sent = payload[0] if len(payload) == 1 else jnp.concatenate(payload, axis=1)
        got = lax.all_to_all(sent, "dp", split_axis=0, concat_axis=0, tiled=True)
        width = 0
        if step < chunk_count:
            neighbour_parts.append(got[:, :chunk_cap].reshape(chunk_slots, NB_LEN, ENC))
            width = chunk_cap
        if step >= 2:
            returned_parts.append(got[:, width:].reshape(chunk_slots, NB_LEN, ENC))
        g = step - 1
        if 0 <= g < chunk_count:
            neighbours = jnp.take(neighbour_parts[g], slot_indices[g], axis=0).reshape(
                chunk_refs * NB_LEN, ENC
            )
            blocks = slice(g * chunk_blocks, (g + 1) * chunk_blocks)
            context_shift, query_shift, proj_grads, near_grads = attend_chunk(
                query_blocks[blocks], grad_blocks[blocks], neighbours, key_weight, value_weight,
                head_count,
            )
            context_parts.append(context_shift)
            query_parts.append(query_shift)
            padded = jnp.concatenate(
                [
                    jnp.zeros((1, NB_LEN, ENC), jnp.bfloat16),
                    near_grads.astype(jnp.bfloat16).reshape(chunk_refs, NB_LEN, ENC),
                ],
                axis=0,
            )
            grads_out.append(jnp.take(padded, slot_refs[g], axis=0))
            seq_major.append(
                neighbours.reshape(chunk_refs * NB_LEN, shard_count, seq_total, enc_share)
                .transpose(0, 2, 1, 3)
                .reshape(chunk_refs * NB_LEN, ENC)
            )
            proj_parts.append(proj_grads)

    def weight_term(first, last):
        return jnp.einsum(
            "px,pz->xz",
            jnp.concatenate(seq_major[first:last], axis=0),
            jnp.concatenate(proj_parts[first:last], axis=0),
            preferred_element_type=jnp.float32,
        )

    weight_terms = weight_term(chunk_count - 1, chunk_count)
    if chunk_count > 1:
        weight_terms = weight_term(0, chunk_count - 1) + weight_terms

    returned = jnp.stack(
        [part.reshape(shard_count, chunk_cap, NB_LEN, ENC) for part in returned_parts], axis=1
    ).reshape(shard_count * chunk_count * chunk_cap, NB_LEN, ENC)
    row_hits = one_hot(arrived.reshape(-1), database.shape[0]).astype(jnp.bfloat16)
    database_grad = jnp.einsum(
        "sr,sax->rax", row_hits, returned, preferred_element_type=jnp.float32
    )

    context_shift = jnp.concatenate(context_parts, axis=0).reshape(seq_count, seq_span, feat_width)
    query_shift = jnp.concatenate(query_parts, axis=0).reshape(seq_count, seq_span, feat_width)
    keep_rows = seq_span - lag_rows
    prior_context, prior_grads = shifted(
        (context_shift[:, keep_rows:], query_shift[:, keep_rows:]), "seq", 1
    )
    context = jnp.concatenate([prior_context, context_shift[:, :keep_rows]], axis=1)
    query_grad = jnp.concatenate([prior_grads, query_shift[:, :keep_rows]], axis=1)

    plane_sums = lax.psum_scatter(
        weight_terms.reshape(seq_total, shard_count * enc_share, 2 * feat_width),
        "seq",
        scatter_dimension=0,
        tiled=True,
    )
    owned_grads = lax.psum_scatter(
        plane_sums.reshape(shard_count, enc_share, 2 * feat_width),
        "dp",
        scatter_dimension=0,
        tiled=True,
    ).reshape(enc_share, 2 * feat_width)
    return (
        context,
        query_grad,
        database_grad,
        owned_grads[:, :feat_width],
        owned_grads[:, feat_width:],
    )


def solution(mesh):
    return jax.shard_map(
        local,
        mesh=mesh,
        in_specs=(
            P("dp", "seq", None),
            P("dp", "seq", None),
            P(("dp", "seq"), None, None),
            P(),
            P(),
            P("dp", "seq", None, None),
            P("dp", "seq", None, None),
        ),
        out_specs=(
            P("dp", "seq", None),
            P("dp", "seq", None),
            P(("dp", "seq"), None, None),
            P(("dp", "seq"), None),
            P(("dp", "seq"), None),
        ),
        check_vma=False,
    )
```

```python
import jax
import jax.numpy as jnp
from jax import lax
from jax.sharding import PartitionSpec as P

HD = 128
ENC = 896
SPAN = 64
NB_LEN = 128
CHUNKS = 4
LEAD = 2


def shifted(array, axis, by):
    count = lax.axis_size(axis)
    pairs = [(i, i + by) for i in range(count) if 0 <= i + by < count]
    return lax.ppermute(array, axis, pairs)


def one_hot(index, count):
    return (index[:, None] == jnp.arange(count, dtype=jnp.int32)[None, :]).astype(jnp.int32)


def attend_chunk(query_blocks, grad_blocks, neighbours, key_weight, value_weight, head_count):
    block_count = query_blocks.shape[0]
    near_len = neighbours.shape[0] // block_count
    key_rows = jnp.dot(neighbours, key_weight, preferred_element_type=jnp.float32).astype(
        jnp.bfloat16
    )
    value_rows = jnp.dot(neighbours, value_weight, preferred_element_type=jnp.float32).astype(
        jnp.bfloat16
    )
    key_heads = key_rows.reshape(block_count, near_len, head_count, HD)
    value_heads = value_rows.reshape(block_count, near_len, head_count, HD)
    score_scale = HD ** (-0.5)
    scores = (
        jnp.einsum("cqhd,ckhd->chqk", query_blocks, key_heads, preferred_element_type=jnp.float32)
        * score_scale
    )
    weights = jnp.exp(scores)
    weights = weights / jnp.sum(weights, axis=-1, keepdims=True)
    weight_half = weights.astype(jnp.bfloat16)
    context_shift = jnp.einsum(
        "chqk,ckhd->cqhd", weight_half, value_heads, preferred_element_type=jnp.float32
    ).astype(jnp.bfloat16)
    prob_grads = jnp.einsum(
        "cqhd,ckhd->chqk", grad_blocks, value_heads, preferred_element_type=jnp.float32
    )
    row_delta = jnp.sum(weights * prob_grads, axis=-1, keepdims=True)
    score_grads = (score_scale * weights * (prob_grads - row_delta)).astype(jnp.bfloat16)
    query_shift = jnp.einsum(
        "chqk,ckhd->cqhd", score_grads, key_heads, preferred_element_type=jnp.float32
    ).astype(jnp.bfloat16)
    key_grads = jnp.einsum(
        "chqk,cqhd->ckhd", score_grads, query_blocks, preferred_element_type=jnp.float32
    ).astype(jnp.bfloat16)
    value_grads = jnp.einsum(
        "chqk,cqhd->ckhd", weight_half, grad_blocks, preferred_element_type=jnp.float32
    ).astype(jnp.bfloat16)
    feat_width = head_count * HD
    proj_grads = jnp.concatenate(
        [
            key_grads.reshape(block_count * near_len, feat_width),
            value_grads.reshape(block_count * near_len, feat_width),
        ],
        axis=1,
    )
    both_weights = jnp.concatenate([key_weight, value_weight], axis=1)
    near_grads = jnp.einsum(
        "pz,xz->px", proj_grads, both_weights, preferred_element_type=jnp.float32
    )
    return context_shift, query_shift, proj_grads, near_grads


def local(queries, d_context, database, key_weight, value_weight, neighbour_shard, neighbour_row):
    seq_count, seq_span, feat_width = queries.shape
    head_count = feat_width // HD
    lag_rows = SPAN - 1
    block_count = seq_count * seq_span // SPAN
    pick_count = neighbour_shard.shape[-1]
    ref_count = block_count * pick_count
    shard_count = lax.axis_size("dp")
    seq_total = lax.axis_size("seq")
    capacity = 2 * ref_count // shard_count
    chunk_count = CHUNKS if block_count % CHUNKS == 0 else 1
    chunk_blocks = block_count // chunk_count
    chunk_refs = chunk_blocks * pick_count
    chunk_cap = min(chunk_blocks, capacity)
    chunk_slots = shard_count * chunk_cap

    target = neighbour_shard.reshape(chunk_count, chunk_refs)
    wanted = neighbour_row.reshape(chunk_count, chunk_refs)
    slot_indices = []
    requests = []
    slot_refs = []
    for g in range(chunk_count):
        owners = one_hot(target[g], shard_count)
        before = jnp.cumsum(owners, axis=0) - owners
        slot_rank = jnp.sum(before * owners, axis=1)
        slot_index = target[g] * chunk_cap + slot_rank
        placed = one_hot(slot_index, chunk_slots)
        requests.append(
            jnp.sum(placed * wanted[g][:, None], axis=0).reshape(shard_count, 1, chunk_cap)
        )
        ref_ids = jnp.arange(1, chunk_refs + 1, dtype=jnp.int32)
        slot_refs.append(jnp.sum(placed * ref_ids[:, None], axis=0))
        slot_indices.append(slot_index)
    request = jnp.concatenate(requests, axis=1)
    arrived = lax.all_to_all(request, "dp", split_axis=0, concat_axis=0, tiled=True)

    head_rows, head_grads = shifted((queries[:, :lag_rows], d_context[:, :lag_rows]), "seq", -1)
    query_blocks = jnp.concatenate([queries[:, lag_rows:], head_rows], axis=1).reshape(
        block_count, SPAN, head_count, HD
    )
    grad_blocks = jnp.concatenate([d_context[:, lag_rows:], head_grads], axis=1).reshape(
        block_count, SPAN, head_count, HD
    )

    enc_share = ENC // (shard_count * seq_total)
    fetched = []
    link = None
    for g in range(chunk_count):
        rows = jnp.take(database, arrived[:, g, :].reshape(chunk_slots), axis=0)
        if link is not None:
            rows, _ = lax.optimization_barrier((rows, link))
        link = lax.all_to_all(rows, "dp", split_axis=0, concat_axis=0, tiled=True)
        fetched.append((rows, link))

    context_parts = []
    query_parts = []
    grads_out = []
    seq_major = []
    proj_parts = []
    for g in range(chunk_count):
        incoming = fetched[g][1]
        if g + 1 < chunk_count:
            incoming, _ = lax.optimization_barrier((incoming, fetched[g + 1][0]))
        neighbours = jnp.take(incoming, slot_indices[g], axis=0).reshape(
            chunk_refs * NB_LEN, ENC
        )
        blocks = slice(g * chunk_blocks, (g + 1) * chunk_blocks)
        context_shift, query_shift, proj_grads, near_grads = attend_chunk(
            query_blocks[blocks], grad_blocks[blocks], neighbours, key_weight, value_weight,
            head_count,
        )
        context_parts.append(context_shift)
        query_parts.append(query_shift)
        padded = jnp.concatenate(
            [
                jnp.zeros((1, NB_LEN, ENC), jnp.bfloat16),
                near_grads.astype(jnp.bfloat16).reshape(chunk_refs, NB_LEN, ENC),
            ],
            axis=0,
        )
        grads_out.append(jnp.take(padded, slot_refs[g], axis=0))
        seq_major.append(
            neighbours.reshape(chunk_refs * NB_LEN, shard_count, seq_total, enc_share)
            .transpose(0, 2, 1, 3)
            .reshape(chunk_refs * NB_LEN, ENC)
        )
        proj_parts.append(proj_grads)

    def weight_term(first, last):
        return jnp.einsum(
            "px,pz->xz",
            jnp.concatenate(seq_major[first:last], axis=0),
            jnp.concatenate(proj_parts[first:last], axis=0),
            preferred_element_type=jnp.float32,
        )

    weight_terms = weight_term(chunk_count - 1, chunk_count)
    if chunk_count > 1:
        weight_terms = weight_term(0, chunk_count - 1) + weight_terms

    database_grad = None
    for g in range(chunk_count):
        sent, _ = lax.optimization_barrier((grads_out[g], link))
        link = lax.all_to_all(sent, "dp", split_axis=0, concat_axis=0, tiled=True)
        row_hits = one_hot(arrived[:, g, :].reshape(chunk_slots), database.shape[0])
        part = jnp.sum(
            row_hits.astype(jnp.float32)[:, :, None, None]
            * link.astype(jnp.float32)[:, None, :, :],
            axis=0,
        )
        database_grad = part if database_grad is None else database_grad + part

    context_shift = jnp.concatenate(context_parts, axis=0).reshape(seq_count, seq_span, feat_width)
    query_shift = jnp.concatenate(query_parts, axis=0).reshape(seq_count, seq_span, feat_width)
    keep_rows = seq_span - lag_rows
    prior_context, prior_grads = shifted(
        (context_shift[:, keep_rows:], query_shift[:, keep_rows:]), "seq", 1
    )
    context = jnp.concatenate([prior_context, context_shift[:, :keep_rows]], axis=1)
    query_grad = jnp.concatenate([prior_grads, query_shift[:, :keep_rows]], axis=1)

    plane_sums = lax.psum_scatter(
        weight_terms.reshape(seq_total, shard_count * enc_share, 2 * feat_width),
        "seq",
        scatter_dimension=0,
        tiled=True,
    )
    owned_grads = lax.psum_scatter(
        plane_sums.reshape(shard_count, enc_share, 2 * feat_width),
        "dp",
        scatter_dimension=0,
        tiled=True,
    ).reshape(enc_share, 2 * feat_width)
    return (
        context,
        query_grad,
        database_grad,
        owned_grads[:, :feat_width],
        owned_grads[:, feat_width:],
    )


def solution(mesh):
    return jax.shard_map(
        local,
        mesh=mesh,
        in_specs=(
            P("dp", "seq", None),
            P("dp", "seq", None),
            P(("dp", "seq"), None, None),
            P(),
            P(),
            P("dp", "seq", None, None),
            P("dp", "seq", None, None),
        ),
        out_specs=(
            P("dp", "seq", None),
            P("dp", "seq", None),
            P(("dp", "seq"), None, None),
            P(("dp", "seq"), None),
            P(("dp", "seq"), None),
        ),
        check_vma=False,
    )
```

```python
import jax
import jax.numpy as jnp
from jax import lax
from jax.experimental import pallas as pl
from jax.experimental.pallas import tpu as pltpu
from jax.sharding import PartitionSpec as P

HD = 128
ENC = 896
SPAN = 64
NB_LEN = 128
CHUNKS = 4
LEAD = 2


def shifted(array, axis, by):
    count = lax.axis_size(axis)
    pairs = [(i, i + by) for i in range(count) if 0 <= i + by < count]
    return lax.ppermute(array, axis, pairs)


def one_hot(index, count):
    return (index[:, None] == jnp.arange(count, dtype=jnp.int32)[None, :]).astype(jnp.int32)


def _row_sum_kernel(rows_ref, *refs):
    part_refs, out_ref = refs[:-1], refs[-1]
    row = pl.program_id(0)
    out_ref[...] = jnp.zeros(out_ref.shape, out_ref.dtype)
    base = 0
    for part in part_refs:

        def body(s, carry, part=part, base=base):
            @pl.when(rows_ref[base + s] == row)
            def _():
                out_ref[0] += part[s].astype(jnp.float32)

            return carry

        lax.fori_loop(0, part.shape[0], body, 0)
        base += part.shape[0]


def row_sums(rows, parts, row_count):
    width = parts[0].shape[1:]
    whole = lambda r, rows_ref: (0, 0, 0)
    return pl.pallas_call(
        _row_sum_kernel,
        grid_spec=pltpu.PrefetchScalarGridSpec(
            num_scalar_prefetch=1,
            grid=(row_count,),
            in_specs=[pl.BlockSpec(p.shape, whole) for p in parts],
            out_specs=pl.BlockSpec((1,) + width, lambda r, rows_ref: (r, 0, 0)),
        ),
        out_shape=jax.ShapeDtypeStruct((row_count,) + width, jnp.float32),
    )(rows, *parts)


def attend_chunk(query_blocks, grad_blocks, neighbours, key_weight, value_weight, head_count):
    block_count = query_blocks.shape[0]
    near_len = neighbours.shape[0] // block_count
    key_rows = jnp.dot(neighbours, key_weight, preferred_element_type=jnp.float32).astype(
        jnp.bfloat16
    )
    value_rows = jnp.dot(neighbours, value_weight, preferred_element_type=jnp.float32).astype(
        jnp.bfloat16
    )
    key_heads = key_rows.reshape(block_count, near_len, head_count, HD)
    value_heads = value_rows.reshape(block_count, near_len, head_count, HD)
    score_scale = HD ** (-0.5)
    scores = (
        jnp.einsum("cqhd,ckhd->chqk", query_blocks, key_heads, preferred_element_type=jnp.float32)
        * score_scale
    )
    weights = jnp.exp(scores)
    weights = weights / jnp.sum(weights, axis=-1, keepdims=True)
    weight_half = weights.astype(jnp.bfloat16)
    context_shift = jnp.einsum(
        "chqk,ckhd->cqhd", weight_half, value_heads, preferred_element_type=jnp.float32
    ).astype(jnp.bfloat16)
    prob_grads = jnp.einsum(
        "cqhd,ckhd->chqk", grad_blocks, value_heads, preferred_element_type=jnp.float32
    )
    row_delta = jnp.sum(weights * prob_grads, axis=-1, keepdims=True)
    score_grads = (score_scale * weights * (prob_grads - row_delta)).astype(jnp.bfloat16)
    query_shift = jnp.einsum(
        "chqk,ckhd->cqhd", score_grads, key_heads, preferred_element_type=jnp.float32
    ).astype(jnp.bfloat16)
    key_grads = jnp.einsum(
        "chqk,cqhd->ckhd", score_grads, query_blocks, preferred_element_type=jnp.float32
    ).astype(jnp.bfloat16)
    value_grads = jnp.einsum(
        "chqk,cqhd->ckhd", weight_half, grad_blocks, preferred_element_type=jnp.float32
    ).astype(jnp.bfloat16)
    feat_width = head_count * HD
    proj_grads = jnp.concatenate(
        [
            key_grads.reshape(block_count * near_len, feat_width),
            value_grads.reshape(block_count * near_len, feat_width),
        ],
        axis=1,
    )
    both_weights = jnp.concatenate([key_weight, value_weight], axis=1)
    near_grads = jnp.einsum(
        "pz,xz->px", proj_grads, both_weights, preferred_element_type=jnp.float32
    )
    return context_shift, query_shift, proj_grads, near_grads


def local(queries, d_context, database, key_weight, value_weight, neighbour_shard, neighbour_row):
    seq_count, seq_span, feat_width = queries.shape
    head_count = feat_width // HD
    lag_rows = SPAN - 1
    block_count = seq_count * seq_span // SPAN
    pick_count = neighbour_shard.shape[-1]
    ref_count = block_count * pick_count
    shard_count = lax.axis_size("dp")
    seq_total = lax.axis_size("seq")
    capacity = 2 * ref_count // shard_count
    chunk_count = CHUNKS if block_count % CHUNKS == 0 else 1
    chunk_blocks = block_count // chunk_count
    chunk_refs = chunk_blocks * pick_count
    chunk_cap = min(chunk_blocks, capacity)
    chunk_slots = shard_count * chunk_cap

    target = neighbour_shard.reshape(chunk_count, chunk_refs)
    wanted = neighbour_row.reshape(chunk_count, chunk_refs)
    slot_indices = []
    requests = []
    slot_refs = []
    for g in range(chunk_count):
        owners = one_hot(target[g], shard_count)
        before = jnp.cumsum(owners, axis=0) - owners
        slot_rank = jnp.sum(before * owners, axis=1)
        slot_index = target[g] * chunk_cap + slot_rank
        placed = one_hot(slot_index, chunk_slots)
        requests.append(
            jnp.sum(placed * wanted[g][:, None], axis=0).reshape(shard_count, 1, chunk_cap)
        )
        ref_ids = jnp.arange(1, chunk_refs + 1, dtype=jnp.int32)
        slot_refs.append(jnp.sum(placed * ref_ids[:, None], axis=0))
        slot_indices.append(slot_index)
    request = jnp.concatenate(requests, axis=1)
    arrived = lax.all_to_all(request, "dp", split_axis=0, concat_axis=0, tiled=True)

    head_rows, head_grads = shifted((queries[:, :lag_rows], d_context[:, :lag_rows]), "seq", -1)
    query_blocks = jnp.concatenate([queries[:, lag_rows:], head_rows], axis=1).reshape(
        block_count, SPAN, head_count, HD
    )
    grad_blocks = jnp.concatenate([d_context[:, lag_rows:], head_grads], axis=1).reshape(
        block_count, SPAN, head_count, HD
    )

    enc_share = ENC // (shard_count * seq_total)
    fetched = []
    link = None
    for g in range(chunk_count):
        rows = jnp.take(database, arrived[:, g, :].reshape(chunk_slots), axis=0)
        if link is not None:
            rows, _ = lax.optimization_barrier((rows, link))
        link = lax.all_to_all(rows, "dp", split_axis=0, concat_axis=0, tiled=True)
        fetched.append((rows, link))

    context_parts = []
    query_parts = []
    grads_out = []
    seq_major = []
    proj_parts = []
    for g in range(chunk_count):
        incoming = fetched[g][1]
        if g + 1 < chunk_count:
            incoming, _ = lax.optimization_barrier((incoming, fetched[g + 1][0]))
        neighbours = jnp.take(incoming, slot_indices[g], axis=0).reshape(
            chunk_refs * NB_LEN, ENC
        )
        blocks = slice(g * chunk_blocks, (g + 1) * chunk_blocks)
        context_shift, query_shift, proj_grads, near_grads = attend_chunk(
            query_blocks[blocks], grad_blocks[blocks], neighbours, key_weight, value_weight,
            head_count,
        )
        context_parts.append(context_shift)
        query_parts.append(query_shift)
        padded = jnp.concatenate(
            [
                jnp.zeros((1, NB_LEN, ENC), jnp.bfloat16),
                near_grads.astype(jnp.bfloat16).reshape(chunk_refs, NB_LEN, ENC),
            ],
            axis=0,
        )
        grads_out.append(jnp.take(padded, slot_refs[g], axis=0))
        seq_major.append(
            neighbours.reshape(chunk_refs * NB_LEN, shard_count, seq_total, enc_share)
            .transpose(0, 2, 1, 3)
            .reshape(chunk_refs * NB_LEN, ENC)
        )
        proj_parts.append(proj_grads)

    def weight_term(first, last):
        return jnp.einsum(
            "px,pz->xz",
            jnp.concatenate(seq_major[first:last], axis=0),
            jnp.concatenate(proj_parts[first:last], axis=0),
            preferred_element_type=jnp.float32,
        )

    weight_terms = weight_term(chunk_count - 1, chunk_count)
    if chunk_count > 1:
        weight_terms = weight_term(0, chunk_count - 1) + weight_terms

    plane_sums = lax.psum_scatter(
        weight_terms.reshape(seq_total, shard_count * enc_share, 2 * feat_width),
        "seq",
        scatter_dimension=0,
        tiled=True,
    )
    returned_parts = []
    for g in range(chunk_count):
        sent, _ = lax.optimization_barrier((grads_out[g], link))
        if g == chunk_count // 2:
            sent, plane_sums = lax.optimization_barrier((sent, plane_sums))
        link = lax.all_to_all(sent, "dp", split_axis=0, concat_axis=0, tiled=True)
        returned_parts.append(link)
    slot_rows = arrived.transpose(1, 0, 2).reshape(-1)
    database_grad = row_sums(slot_rows, returned_parts, database.shape[0])

    context_shift = jnp.concatenate(context_parts, axis=0).reshape(seq_count, seq_span, feat_width)
    query_shift = jnp.concatenate(query_parts, axis=0).reshape(seq_count, seq_span, feat_width)
    keep_rows = seq_span - lag_rows
    prior_context, prior_grads = shifted(
        (context_shift[:, keep_rows:], query_shift[:, keep_rows:]), "seq", 1
    )
    context = jnp.concatenate([prior_context, context_shift[:, :keep_rows]], axis=1)
    query_grad = jnp.concatenate([prior_grads, query_shift[:, :keep_rows]], axis=1)

    owned_grads = lax.psum_scatter(
        plane_sums.reshape(shard_count, enc_share, 2 * feat_width),
        "dp",
        scatter_dimension=0,
        tiled=True,
    ).reshape(enc_share, 2 * feat_width)
    return (
        context,
        query_grad,
        database_grad,
        owned_grads[:, :feat_width],
        owned_grads[:, feat_width:],
    )


def solution(mesh):
    return jax.shard_map(
        local,
        mesh=mesh,
        in_specs=(
            P("dp", "seq", None),
            P("dp", "seq", None),
            P(("dp", "seq"), None, None),
            P(),
            P(),
            P("dp", "seq", None, None),
            P("dp", "seq", None, None),
        ),
        out_specs=(
            P("dp", "seq", None),
            P("dp", "seq", None),
            P(("dp", "seq"), None, None),
            P(("dp", "seq"), None),
            P(("dp", "seq"), None),
        ),
        check_vma=False,
    )
```

```python
import jax
import jax.numpy as jnp
from jax import lax
from jax.experimental import pallas as pl
from jax.experimental.pallas import tpu as pltpu
from jax.sharding import PartitionSpec as P

HD = 128
ENC = 896
SPAN = 64
NB_LEN = 128
CHUNKS = 4
LEAD = 2


def shifted(array, axis, by):
    count = lax.axis_size(axis)
    pairs = [(i, i + by) for i in range(count) if 0 <= i + by < count]
    return lax.ppermute(array, axis, pairs)


def one_hot(index, count):
    return (index[:, None] == jnp.arange(count, dtype=jnp.int32)[None, :]).astype(jnp.int32)


def _row_sum_kernel(rows_ref, *refs):
    part_refs, out_ref = refs[:-1], refs[-1]
    row = pl.program_id(0)
    out_ref[...] = jnp.zeros(out_ref.shape, out_ref.dtype)
    base = 0
    for part in part_refs:

        def body(s, carry, part=part, base=base):
            @pl.when(rows_ref[base + s] == row)
            def _():
                out_ref[0] += part[s].astype(jnp.float32)

            return carry

        lax.fori_loop(0, part.shape[0], body, 0)
        base += part.shape[0]


def row_sums(rows, parts, row_count):
    width = parts[0].shape[1:]
    whole = lambda r, rows_ref: (0, 0, 0)
    return pl.pallas_call(
        _row_sum_kernel,
        grid_spec=pltpu.PrefetchScalarGridSpec(
            num_scalar_prefetch=1,
            grid=(row_count,),
            in_specs=[pl.BlockSpec(p.shape, whole) for p in parts],
            out_specs=pl.BlockSpec((1,) + width, lambda r, rows_ref: (r, 0, 0)),
        ),
        out_shape=jax.ShapeDtypeStruct((row_count,) + width, jnp.float32),
    )(rows, *parts)


def attend_chunk(query_blocks, grad_blocks, neighbours, key_weight, value_weight, head_count):
    block_count = query_blocks.shape[0]
    near_len = neighbours.shape[0] // block_count
    key_rows = jnp.dot(neighbours, key_weight, preferred_element_type=jnp.float32).astype(
        jnp.bfloat16
    )
    value_rows = jnp.dot(neighbours, value_weight, preferred_element_type=jnp.float32).astype(
        jnp.bfloat16
    )
    key_heads = key_rows.reshape(block_count, near_len, head_count, HD)
    value_heads = value_rows.reshape(block_count, near_len, head_count, HD)
    score_scale = HD ** (-0.5)
    scores = (
        jnp.einsum("cqhd,ckhd->chqk", query_blocks, key_heads, preferred_element_type=jnp.float32)
        * score_scale
    )
    weights = jnp.exp(scores)
    weights = weights / jnp.sum(weights, axis=-1, keepdims=True)
    weight_half = weights.astype(jnp.bfloat16)
    context_shift = jnp.einsum(
        "chqk,ckhd->cqhd", weight_half, value_heads, preferred_element_type=jnp.float32
    ).astype(jnp.bfloat16)
    prob_grads = jnp.einsum(
        "cqhd,ckhd->chqk", grad_blocks, value_heads, preferred_element_type=jnp.float32
    )
    row_delta = jnp.sum(weights * prob_grads, axis=-1, keepdims=True)
    score_grads = (score_scale * weights * (prob_grads - row_delta)).astype(jnp.bfloat16)
    query_shift = jnp.einsum(
        "chqk,ckhd->cqhd", score_grads, key_heads, preferred_element_type=jnp.float32
    ).astype(jnp.bfloat16)
    key_grads = jnp.einsum(
        "chqk,cqhd->ckhd", score_grads, query_blocks, preferred_element_type=jnp.float32
    ).astype(jnp.bfloat16)
    value_grads = jnp.einsum(
        "chqk,cqhd->ckhd", weight_half, grad_blocks, preferred_element_type=jnp.float32
    ).astype(jnp.bfloat16)
    feat_width = head_count * HD
    proj_grads = jnp.concatenate(
        [
            key_grads.reshape(block_count * near_len, feat_width),
            value_grads.reshape(block_count * near_len, feat_width),
        ],
        axis=1,
    )
    both_weights = jnp.concatenate([key_weight, value_weight], axis=1)
    near_grads = jnp.einsum(
        "pz,xz->px", proj_grads, both_weights, preferred_element_type=jnp.float32
    )
    return context_shift, query_shift, proj_grads, near_grads


def local(queries, d_context, database, key_weight, value_weight, neighbour_shard, neighbour_row):
    seq_count, seq_span, feat_width = queries.shape
    head_count = feat_width // HD
    lag_rows = SPAN - 1
    block_count = seq_count * seq_span // SPAN
    pick_count = neighbour_shard.shape[-1]
    ref_count = block_count * pick_count
    shard_count = lax.axis_size("dp")
    seq_total = lax.axis_size("seq")
    capacity = 2 * ref_count // shard_count
    chunk_count = CHUNKS if block_count % CHUNKS == 0 else 1
    chunk_blocks = block_count // chunk_count
    chunk_refs = chunk_blocks * pick_count
    chunk_cap = min(chunk_blocks, capacity)
    chunk_slots = shard_count * chunk_cap

    target = neighbour_shard.reshape(chunk_count, chunk_refs)
    wanted = neighbour_row.reshape(chunk_count, chunk_refs)
    slot_indices = []
    requests = []
    slot_refs = []
    for g in range(chunk_count):
        owners = one_hot(target[g], shard_count)
        before = jnp.cumsum(owners, axis=0) - owners
        slot_rank = jnp.sum(before * owners, axis=1)
        slot_index = target[g] * chunk_cap + slot_rank
        placed = one_hot(slot_index, chunk_slots)
        requests.append(
            jnp.sum(placed * wanted[g][:, None], axis=0).reshape(shard_count, 1, chunk_cap)
        )
        ref_ids = jnp.arange(1, chunk_refs + 1, dtype=jnp.int32)
        slot_refs.append(jnp.sum(placed * ref_ids[:, None], axis=0))
        slot_indices.append(slot_index)
    request = jnp.concatenate(requests, axis=1)
    arrived = lax.all_to_all(request, "dp", split_axis=0, concat_axis=0, tiled=True)

    head_rows, head_grads = shifted((queries[:, :lag_rows], d_context[:, :lag_rows]), "seq", -1)
    query_blocks = jnp.concatenate([queries[:, lag_rows:], head_rows], axis=1).reshape(
        block_count, SPAN, head_count, HD
    )
    grad_blocks = jnp.concatenate([d_context[:, lag_rows:], head_grads], axis=1).reshape(
        block_count, SPAN, head_count, HD
    )

    enc_share = ENC // (shard_count * seq_total)
    fetched = []
    link = None
    for g in range(chunk_count):
        rows = jnp.take(database, arrived[:, g, :].reshape(chunk_slots), axis=0)
        if link is not None:
            rows, _ = lax.optimization_barrier((rows, link))
        link = lax.all_to_all(rows, "dp", split_axis=0, concat_axis=0, tiled=True)
        fetched.append((rows, link))

    context_parts = []
    query_parts = []
    returned_parts = []
    grads_out = []
    seq_major = []
    proj_parts = []

    def weight_term(first, last):
        return jnp.einsum(
            "px,pz->xz",
            jnp.concatenate(seq_major[first:last], axis=0),
            jnp.concatenate(proj_parts[first:last], axis=0),
            preferred_element_type=jnp.float32,
        )

    for g in range(chunk_count):
        incoming = fetched[g][1]
        if g + 1 < chunk_count:
            incoming, _ = lax.optimization_barrier((incoming, fetched[g + 1][0]))
        if g >= 1:
            incoming, _ = lax.optimization_barrier((incoming, grads_out[g - 1]))
        if g >= 1 and g == chunk_count - 1:
            early_terms = weight_term(0, g)
            sent, _ = lax.optimization_barrier((grads_out[0], link))
            link = lax.all_to_all(sent, "dp", split_axis=0, concat_axis=0, tiled=True)
            returned_parts.append(link)
            incoming, early_terms, _ = lax.optimization_barrier((incoming, early_terms, sent))
        neighbours = jnp.take(incoming, slot_indices[g], axis=0).reshape(
            chunk_refs * NB_LEN, ENC
        )
        blocks = slice(g * chunk_blocks, (g + 1) * chunk_blocks)
        context_shift, query_shift, proj_grads, near_grads = attend_chunk(
            query_blocks[blocks], grad_blocks[blocks], neighbours, key_weight, value_weight,
            head_count,
        )
        context_parts.append(context_shift)
        query_parts.append(query_shift)
        padded = jnp.concatenate(
            [
                jnp.zeros((1, NB_LEN, ENC), jnp.bfloat16),
                near_grads.astype(jnp.bfloat16).reshape(chunk_refs, NB_LEN, ENC),
            ],
            axis=0,
        )
        grads_out.append(jnp.take(padded, slot_refs[g], axis=0))
        seq_major.append(
            neighbours.reshape(chunk_refs * NB_LEN, shard_count, seq_total, enc_share)
            .transpose(0, 2, 1, 3)
            .reshape(chunk_refs * NB_LEN, ENC)
        )
        proj_parts.append(proj_grads)

    weight_terms = weight_term(chunk_count - 1, chunk_count)
    if chunk_count > 1:
        weight_terms = early_terms + weight_terms

    plane_sums = lax.psum_scatter(
        weight_terms.reshape(seq_total, shard_count * enc_share, 2 * feat_width),
        "seq",
        scatter_dimension=0,
        tiled=True,
    )
    for g in range(len(returned_parts), chunk_count):
        sent, _ = lax.optimization_barrier((grads_out[g], link))
        if g == chunk_count // 2:
            sent, plane_sums = lax.optimization_barrier((sent, plane_sums))
        link = lax.all_to_all(sent, "dp", split_axis=0, concat_axis=0, tiled=True)
        returned_parts.append(link)
    slot_rows = arrived.transpose(1, 0, 2).reshape(-1)
    database_grad = row_sums(slot_rows, returned_parts, database.shape[0])

    context_shift = jnp.concatenate(context_parts, axis=0).reshape(seq_count, seq_span, feat_width)
    query_shift = jnp.concatenate(query_parts, axis=0).reshape(seq_count, seq_span, feat_width)
    keep_rows = seq_span - lag_rows
    prior_context, prior_grads = shifted(
        (context_shift[:, keep_rows:], query_shift[:, keep_rows:]), "seq", 1
    )
    context = jnp.concatenate([prior_context, context_shift[:, :keep_rows]], axis=1)
    query_grad = jnp.concatenate([prior_grads, query_shift[:, :keep_rows]], axis=1)

    owned_grads = lax.psum_scatter(
        plane_sums.reshape(shard_count, enc_share, 2 * feat_width),
        "dp",
        scatter_dimension=0,
        tiled=True,
    ).reshape(enc_share, 2 * feat_width)
    return (
        context,
        query_grad,
        database_grad,
        owned_grads[:, :feat_width],
        owned_grads[:, feat_width:],
    )


def solution(mesh):
    return jax.shard_map(
        local,
        mesh=mesh,
        in_specs=(
            P("dp", "seq", None),
            P("dp", "seq", None),
            P(("dp", "seq"), None, None),
            P(),
            P(),
            P("dp", "seq", None, None),
            P("dp", "seq", None, None),
        ),
        out_specs=(
            P("dp", "seq", None),
            P("dp", "seq", None),
            P(("dp", "seq"), None, None),
            P(("dp", "seq"), None),
            P(("dp", "seq"), None),
        ),
        check_vma=False,
    )
```

```python
import jax
import jax.numpy as jnp
from jax import lax
from jax.experimental import pallas as pl
from jax.experimental.pallas import tpu as pltpu
from jax.sharding import PartitionSpec as P

HD = 128
ENC = 896
SPAN = 64
NB_LEN = 128
CHUNKS = 4
LEAD = 2


def shifted(array, axis, by):
    count = lax.axis_size(axis)
    pairs = [(i, i + by) for i in range(count) if 0 <= i + by < count]
    return lax.ppermute(array, axis, pairs)


def one_hot(index, count):
    return (index[:, None] == jnp.arange(count, dtype=jnp.int32)[None, :]).astype(jnp.int32)


def _row_sum_kernel(rows_ref, *refs):
    part_refs, out_ref = refs[:-1], refs[-1]
    block_rows = out_ref.shape[0]
    first = pl.program_id(0) * block_rows
    out_ref[...] = jnp.zeros(out_ref.shape, out_ref.dtype)
    base = 0
    for part in part_refs:

        def body(s, carry, part=part, base=base):
            local = rows_ref[base + s] - first

            @pl.when((local >= 0) & (local < block_rows))
            def _():
                out_ref[local] += part[s].astype(jnp.float32)

            return carry

        lax.fori_loop(0, part.shape[0], body, 0)
        base += part.shape[0]


def row_sums(rows, parts, row_count):
    width = parts[0].shape[1:]
    block_rows = 8 if row_count % 8 == 0 else row_count
    whole = lambda r, rows_ref: (0, 0, 0)
    return pl.pallas_call(
        _row_sum_kernel,
        grid_spec=pltpu.PrefetchScalarGridSpec(
            num_scalar_prefetch=1,
            grid=(row_count // block_rows,),
            in_specs=[pl.BlockSpec(p.shape, whole) for p in parts],
            out_specs=pl.BlockSpec((block_rows,) + width, lambda r, rows_ref: (r, 0, 0)),
        ),
        out_shape=jax.ShapeDtypeStruct((row_count,) + width, jnp.float32),
    )(rows, *parts)


def attend_chunk(query_blocks, grad_blocks, neighbours, key_weight, value_weight, head_count):
    block_count = query_blocks.shape[0]
    near_len = neighbours.shape[0] // block_count
    key_rows = jnp.dot(neighbours, key_weight, preferred_element_type=jnp.float32).astype(
        jnp.bfloat16
    )
    value_rows = jnp.dot(neighbours, value_weight, preferred_element_type=jnp.float32).astype(
        jnp.bfloat16
    )
    key_heads = key_rows.reshape(block_count, near_len, head_count, HD)
    value_heads = value_rows.reshape(block_count, near_len, head_count, HD)
    score_scale = HD ** (-0.5)
    scores = (
        jnp.einsum("cqhd,ckhd->chqk", query_blocks, key_heads, preferred_element_type=jnp.float32)
        * score_scale
    )
    weights = jnp.exp(scores)
    weights = weights / jnp.sum(weights, axis=-1, keepdims=True)
    weight_half = weights.astype(jnp.bfloat16)
    context_shift = jnp.einsum(
        "chqk,ckhd->cqhd", weight_half, value_heads, preferred_element_type=jnp.float32
    ).astype(jnp.bfloat16)
    prob_grads = jnp.einsum(
        "cqhd,ckhd->chqk", grad_blocks, value_heads, preferred_element_type=jnp.float32
    )
    row_delta = jnp.sum(weights * prob_grads, axis=-1, keepdims=True)
    score_grads = (score_scale * weights * (prob_grads - row_delta)).astype(jnp.bfloat16)
    query_shift = jnp.einsum(
        "chqk,ckhd->cqhd", score_grads, key_heads, preferred_element_type=jnp.float32
    ).astype(jnp.bfloat16)
    key_grads = jnp.einsum(
        "chqk,cqhd->ckhd", score_grads, query_blocks, preferred_element_type=jnp.float32
    ).astype(jnp.bfloat16)
    value_grads = jnp.einsum(
        "chqk,cqhd->ckhd", weight_half, grad_blocks, preferred_element_type=jnp.float32
    ).astype(jnp.bfloat16)
    feat_width = head_count * HD
    proj_grads = jnp.concatenate(
        [
            key_grads.reshape(block_count * near_len, feat_width),
            value_grads.reshape(block_count * near_len, feat_width),
        ],
        axis=1,
    )
    both_weights = jnp.concatenate([key_weight, value_weight], axis=1)
    near_grads = jnp.einsum(
        "pz,xz->px", proj_grads, both_weights, preferred_element_type=jnp.float32
    )
    return context_shift, query_shift, proj_grads, near_grads


def local(queries, d_context, database, key_weight, value_weight, neighbour_shard, neighbour_row):
    seq_count, seq_span, feat_width = queries.shape
    head_count = feat_width // HD
    lag_rows = SPAN - 1
    block_count = seq_count * seq_span // SPAN
    pick_count = neighbour_shard.shape[-1]
    ref_count = block_count * pick_count
    shard_count = lax.axis_size("dp")
    seq_total = lax.axis_size("seq")
    capacity = 2 * ref_count // shard_count
    chunk_count = CHUNKS if block_count % CHUNKS == 0 else 1
    chunk_blocks = block_count // chunk_count
    chunk_refs = chunk_blocks * pick_count
    chunk_cap = min(chunk_blocks, capacity)
    chunk_slots = shard_count * chunk_cap

    target = neighbour_shard.reshape(chunk_count, chunk_refs)
    wanted = neighbour_row.reshape(chunk_count, chunk_refs)
    slot_indices = []
    requests = []
    slot_refs = []
    for g in range(chunk_count):
        owners = one_hot(target[g], shard_count)
        before = jnp.cumsum(owners, axis=0) - owners
        slot_rank = jnp.sum(before * owners, axis=1)
        slot_index = target[g] * chunk_cap + slot_rank
        placed = one_hot(slot_index, chunk_slots)
        requests.append(
            jnp.sum(placed * wanted[g][:, None], axis=0).reshape(shard_count, 1, chunk_cap)
        )
        ref_ids = jnp.arange(1, chunk_refs + 1, dtype=jnp.int32)
        slot_refs.append(jnp.sum(placed * ref_ids[:, None], axis=0))
        slot_indices.append(slot_index)
    request = jnp.concatenate(requests, axis=1)
    arrived = lax.all_to_all(request, "dp", split_axis=0, concat_axis=0, tiled=True)

    head_rows, head_grads = shifted((queries[:, :lag_rows], d_context[:, :lag_rows]), "seq", -1)
    query_blocks = jnp.concatenate([queries[:, lag_rows:], head_rows], axis=1).reshape(
        block_count, SPAN, head_count, HD
    )
    grad_blocks = jnp.concatenate([d_context[:, lag_rows:], head_grads], axis=1).reshape(
        block_count, SPAN, head_count, HD
    )

    enc_share = ENC // (shard_count * seq_total)
    fetched = []
    link = None
    for g in range(chunk_count):
        rows = jnp.take(database, arrived[:, g, :].reshape(chunk_slots), axis=0)
        if link is not None:
            rows, _ = lax.optimization_barrier((rows, link))
        link = lax.all_to_all(rows, "dp", split_axis=0, concat_axis=0, tiled=True)
        fetched.append((rows, link))

    context_parts = []
    query_parts = []
    grads_out = []
    seq_major = []
    proj_parts = []
    for g in range(chunk_count):
        incoming = fetched[g][1]
        if g + 1 < chunk_count:
            incoming, _ = lax.optimization_barrier((incoming, fetched[g + 1][0]))
        neighbours = jnp.take(incoming, slot_indices[g], axis=0).reshape(
            chunk_refs * NB_LEN, ENC
        )
        blocks = slice(g * chunk_blocks, (g + 1) * chunk_blocks)
        context_shift, query_shift, proj_grads, near_grads = attend_chunk(
            query_blocks[blocks], grad_blocks[blocks], neighbours, key_weight, value_weight,
            head_count,
        )
        context_parts.append(context_shift)
        query_parts.append(query_shift)
        padded = jnp.concatenate(
            [
                jnp.zeros((1, NB_LEN, ENC), jnp.bfloat16),
                near_grads.astype(jnp.bfloat16).reshape(chunk_refs, NB_LEN, ENC),
            ],
            axis=0,
        )
        grads_out.append(jnp.take(padded, slot_refs[g], axis=0))
        seq_major.append(
            neighbours.reshape(chunk_refs * NB_LEN, shard_count, seq_total, enc_share)
            .transpose(0, 2, 1, 3)
            .reshape(chunk_refs * NB_LEN, ENC)
        )
        proj_parts.append(proj_grads)

    def weight_term(first, last):
        return jnp.einsum(
            "px,pz->xz",
            jnp.concatenate(seq_major[first:last], axis=0),
            jnp.concatenate(proj_parts[first:last], axis=0),
            preferred_element_type=jnp.float32,
        )

    weight_terms = weight_term(chunk_count - 1, chunk_count)
    if chunk_count > 1:
        weight_terms = weight_term(0, chunk_count - 1) + weight_terms

    plane_sums = lax.psum_scatter(
        weight_terms.reshape(seq_total, shard_count * enc_share, 2 * feat_width),
        "seq",
        scatter_dimension=0,
        tiled=True,
    )
    returned_parts = []
    for g in range(chunk_count):
        sent, _ = lax.optimization_barrier((grads_out[g], link))
        if g == chunk_count // 2:
            sent, plane_sums = lax.optimization_barrier((sent, plane_sums))
        link = lax.all_to_all(sent, "dp", split_axis=0, concat_axis=0, tiled=True)
        returned_parts.append(link)
    slot_rows = arrived.transpose(1, 0, 2).reshape(-1)
    database_grad = row_sums(slot_rows, returned_parts, database.shape[0])

    context_shift = jnp.concatenate(context_parts, axis=0).reshape(seq_count, seq_span, feat_width)
    query_shift = jnp.concatenate(query_parts, axis=0).reshape(seq_count, seq_span, feat_width)
    keep_rows = seq_span - lag_rows
    prior_context, prior_grads = shifted(
        (context_shift[:, keep_rows:], query_shift[:, keep_rows:]), "seq", 1
    )
    context = jnp.concatenate([prior_context, context_shift[:, :keep_rows]], axis=1)
    query_grad = jnp.concatenate([prior_grads, query_shift[:, :keep_rows]], axis=1)

    owned_grads = lax.psum_scatter(
        plane_sums.reshape(shard_count, enc_share, 2 * feat_width),
        "dp",
        scatter_dimension=0,
        tiled=True,
    ).reshape(enc_share, 2 * feat_width)
    return (
        context,
        query_grad,
        database_grad,
        owned_grads[:, :feat_width],
        owned_grads[:, feat_width:],
    )


def solution(mesh):
    return jax.shard_map(
        local,
        mesh=mesh,
        in_specs=(
            P("dp", "seq", None),
            P("dp", "seq", None),
            P(("dp", "seq"), None, None),
            P(),
            P(),
            P("dp", "seq", None, None),
            P("dp", "seq", None, None),
        ),
        out_specs=(
            P("dp", "seq", None),
            P("dp", "seq", None),
            P(("dp", "seq"), None, None),
            P(("dp", "seq"), None),
            P(("dp", "seq"), None),
        ),
        check_vma=False,
    )
```

```python
import jax
import jax.numpy as jnp
from jax import lax
from jax.experimental import pallas as pl
from jax.experimental.pallas import tpu as pltpu
from jax.sharding import PartitionSpec as P

HD = 128
ENC = 896
SPAN = 64
NB_LEN = 128
CHUNKS = 4
LEAD = 2


def shifted(array, axis, by):
    count = lax.axis_size(axis)
    pairs = [(i, i + by) for i in range(count) if 0 <= i + by < count]
    return lax.ppermute(array, axis, pairs)


def one_hot(index, count):
    return (index[:, None] == jnp.arange(count, dtype=jnp.int32)[None, :]).astype(jnp.int32)


def _row_sum_kernel(rows_ref, *refs):
    part_refs, out_ref = refs[:-1], refs[-1]
    block_rows = out_ref.shape[0]
    first = pl.program_id(0) * block_rows
    out_ref[...] = jnp.zeros(out_ref.shape, out_ref.dtype)
    base = 0
    for part in part_refs:

        def body(s, carry, part=part, base=base):
            local = rows_ref[base + s] - first

            @pl.when((local >= 0) & (local < block_rows))
            def _():
                out_ref[local] += part[s].astype(jnp.float32)

            return carry

        lax.fori_loop(0, part.shape[0], body, 0)
        base += part.shape[0]


def row_sums(rows, parts, row_count):
    width = parts[0].shape[1:]
    block_rows = 8 if row_count % 8 == 0 else row_count
    whole = lambda r, rows_ref: (0, 0, 0)
    return pl.pallas_call(
        _row_sum_kernel,
        grid_spec=pltpu.PrefetchScalarGridSpec(
            num_scalar_prefetch=1,
            grid=(row_count // block_rows,),
            in_specs=[pl.BlockSpec(p.shape, whole) for p in parts],
            out_specs=pl.BlockSpec((block_rows,) + width, lambda r, rows_ref: (r, 0, 0)),
        ),
        out_shape=jax.ShapeDtypeStruct((row_count,) + width, jnp.float32),
    )(rows, *parts)


def attend_chunk(query_blocks, grad_blocks, neighbours, key_weight, value_weight, head_count):
    block_count = query_blocks.shape[0]
    near_len = neighbours.shape[0] // block_count
    key_rows = jnp.dot(neighbours, key_weight, preferred_element_type=jnp.float32).astype(
        jnp.bfloat16
    )
    value_rows = jnp.dot(neighbours, value_weight, preferred_element_type=jnp.float32).astype(
        jnp.bfloat16
    )
    key_heads = key_rows.reshape(block_count, near_len, head_count, HD)
    value_heads = value_rows.reshape(block_count, near_len, head_count, HD)
    score_scale = HD ** (-0.5)
    scores = (
        jnp.einsum("cqhd,ckhd->chqk", query_blocks, key_heads, preferred_element_type=jnp.float32)
        * score_scale
    )
    weights = jnp.exp(scores)
    weights = weights / jnp.sum(weights, axis=-1, keepdims=True)
    weight_half = weights.astype(jnp.bfloat16)
    context_shift = jnp.einsum(
        "chqk,ckhd->cqhd", weight_half, value_heads, preferred_element_type=jnp.float32
    ).astype(jnp.bfloat16)
    prob_grads = jnp.einsum(
        "cqhd,ckhd->chqk", grad_blocks, value_heads, preferred_element_type=jnp.float32
    )
    row_delta = jnp.sum(weights * prob_grads, axis=-1, keepdims=True)
    score_grads = (score_scale * weights * (prob_grads - row_delta)).astype(jnp.bfloat16)
    query_shift = jnp.einsum(
        "chqk,ckhd->cqhd", score_grads, key_heads, preferred_element_type=jnp.float32
    ).astype(jnp.bfloat16)
    key_grads = jnp.einsum(
        "chqk,cqhd->ckhd", score_grads, query_blocks, preferred_element_type=jnp.float32
    ).astype(jnp.bfloat16)
    value_grads = jnp.einsum(
        "chqk,cqhd->ckhd", weight_half, grad_blocks, preferred_element_type=jnp.float32
    ).astype(jnp.bfloat16)
    feat_width = head_count * HD
    proj_grads = jnp.concatenate(
        [
            key_grads.reshape(block_count * near_len, feat_width),
            value_grads.reshape(block_count * near_len, feat_width),
        ],
        axis=1,
    )
    both_weights = jnp.concatenate([key_weight, value_weight], axis=1)
    near_grads = jnp.einsum(
        "pz,xz->px", proj_grads, both_weights, preferred_element_type=jnp.float32
    )
    return context_shift, query_shift, proj_grads, near_grads


def local(queries, d_context, database, key_weight, value_weight, neighbour_shard, neighbour_row):
    seq_count, seq_span, feat_width = queries.shape
    head_count = feat_width // HD
    lag_rows = SPAN - 1
    block_count = seq_count * seq_span // SPAN
    pick_count = neighbour_shard.shape[-1]
    ref_count = block_count * pick_count
    shard_count = lax.axis_size("dp")
    seq_total = lax.axis_size("seq")
    capacity = 2 * ref_count // shard_count
    chunk_count = CHUNKS if block_count % CHUNKS == 0 else 1
    chunk_blocks = block_count // chunk_count
    chunk_refs = chunk_blocks * pick_count
    chunk_cap = min(chunk_blocks, capacity)
    chunk_slots = shard_count * chunk_cap

    target = neighbour_shard.reshape(chunk_count, chunk_refs)
    wanted = neighbour_row.reshape(chunk_count, chunk_refs)
    slot_indices = []
    requests = []
    slot_refs = []
    for g in range(chunk_count):
        owners = one_hot(target[g], shard_count)
        before = jnp.cumsum(owners, axis=0) - owners
        slot_rank = jnp.sum(before * owners, axis=1)
        slot_index = target[g] * chunk_cap + slot_rank
        placed = one_hot(slot_index, chunk_slots)
        requests.append(
            jnp.sum(placed * wanted[g][:, None], axis=0).reshape(shard_count, 1, chunk_cap)
        )
        ref_ids = jnp.arange(1, chunk_refs + 1, dtype=jnp.int32)
        slot_refs.append(jnp.sum(placed * ref_ids[:, None], axis=0))
        slot_indices.append(slot_index)
    request = jnp.concatenate(requests, axis=1)
    arrived = lax.all_to_all(request, "dp", split_axis=0, concat_axis=0, tiled=True)

    head_rows, head_grads = shifted((queries[:, :lag_rows], d_context[:, :lag_rows]), "seq", -1)
    query_blocks = jnp.concatenate([queries[:, lag_rows:], head_rows], axis=1).reshape(
        block_count, SPAN, head_count, HD
    )
    grad_blocks = jnp.concatenate([d_context[:, lag_rows:], head_grads], axis=1).reshape(
        block_count, SPAN, head_count, HD
    )

    enc_share = ENC // (shard_count * seq_total)
    fetched = []
    link = None
    for g in range(chunk_count):
        rows = jnp.take(database, arrived[:, g, :].reshape(chunk_slots), axis=0)
        if link is not None:
            rows, _ = lax.optimization_barrier((rows, link))
        link = lax.all_to_all(rows, "dp", split_axis=0, concat_axis=0, tiled=True)
        fetched.append((rows, link))

    context_parts = []
    query_parts = []
    returned_parts = []
    grads_out = []
    seq_major = []
    proj_parts = []
    for g in range(chunk_count):
        incoming = fetched[g][1]
        if g + 1 < chunk_count:
            incoming, _ = lax.optimization_barrier((incoming, fetched[g + 1][0]))
        if g >= 1:
            incoming, _ = lax.optimization_barrier((incoming, grads_out[g - 1]))
        if g >= 1 and g == chunk_count - 1:
            sent, _ = lax.optimization_barrier((grads_out[0], link))
            link = lax.all_to_all(sent, "dp", split_axis=0, concat_axis=0, tiled=True)
            returned_parts.append(link)
            incoming, _ = lax.optimization_barrier((incoming, link))
        neighbours = jnp.take(incoming, slot_indices[g], axis=0).reshape(
            chunk_refs * NB_LEN, ENC
        )
        blocks = slice(g * chunk_blocks, (g + 1) * chunk_blocks)
        context_shift, query_shift, proj_grads, near_grads = attend_chunk(
            query_blocks[blocks], grad_blocks[blocks], neighbours, key_weight, value_weight,
            head_count,
        )
        context_parts.append(context_shift)
        query_parts.append(query_shift)
        padded = jnp.concatenate(
            [
                jnp.zeros((1, NB_LEN, ENC), jnp.bfloat16),
                near_grads.astype(jnp.bfloat16).reshape(chunk_refs, NB_LEN, ENC),
            ],
            axis=0,
        )
        grads_out.append(jnp.take(padded, slot_refs[g], axis=0))
        seq_major.append(
            neighbours.reshape(chunk_refs * NB_LEN, shard_count, seq_total, enc_share)
            .transpose(0, 2, 1, 3)
            .reshape(chunk_refs * NB_LEN, ENC)
        )
        proj_parts.append(proj_grads)

    def weight_term(first, last):
        return jnp.einsum(
            "px,pz->xz",
            jnp.concatenate(seq_major[first:last], axis=0),
            jnp.concatenate(proj_parts[first:last], axis=0),
            preferred_element_type=jnp.float32,
        )

    weight_terms = weight_term(chunk_count - 1, chunk_count)
    if chunk_count > 1:
        weight_terms = weight_term(0, chunk_count - 1) + weight_terms

    plane_sums = lax.psum_scatter(
        weight_terms.reshape(seq_total, shard_count * enc_share, 2 * feat_width),
        "seq",
        scatter_dimension=0,
        tiled=True,
    )
    for g in range(len(returned_parts), chunk_count):
        sent, _ = lax.optimization_barrier((grads_out[g], link))
        if g == chunk_count // 2:
            sent, plane_sums = lax.optimization_barrier((sent, plane_sums))
        link = lax.all_to_all(sent, "dp", split_axis=0, concat_axis=0, tiled=True)
        returned_parts.append(link)
    slot_rows = arrived.transpose(1, 0, 2).reshape(-1)
    database_grad = row_sums(slot_rows, returned_parts, database.shape[0])

    context_shift = jnp.concatenate(context_parts, axis=0).reshape(seq_count, seq_span, feat_width)
    query_shift = jnp.concatenate(query_parts, axis=0).reshape(seq_count, seq_span, feat_width)
    keep_rows = seq_span - lag_rows
    prior_context, prior_grads = shifted(
        (context_shift[:, keep_rows:], query_shift[:, keep_rows:]), "seq", 1
    )
    context = jnp.concatenate([prior_context, context_shift[:, :keep_rows]], axis=1)
    query_grad = jnp.concatenate([prior_grads, query_shift[:, :keep_rows]], axis=1)

    owned_grads = lax.psum_scatter(
        plane_sums.reshape(shard_count, enc_share, 2 * feat_width),
        "dp",
        scatter_dimension=0,
        tiled=True,
    ).reshape(enc_share, 2 * feat_width)
    return (
        context,
        query_grad,
        database_grad,
        owned_grads[:, :feat_width],
        owned_grads[:, feat_width:],
    )


def solution(mesh):
    return jax.shard_map(
        local,
        mesh=mesh,
        in_specs=(
            P("dp", "seq", None),
            P("dp", "seq", None),
            P(("dp", "seq"), None, None),
            P(),
            P(),
            P("dp", "seq", None, None),
            P("dp", "seq", None, None),
        ),
        out_specs=(
            P("dp", "seq", None),
            P("dp", "seq", None),
            P(("dp", "seq"), None, None),
            P(("dp", "seq"), None),
            P(("dp", "seq"), None),
        ),
        check_vma=False,
    )
```

```python
import jax
import jax.numpy as jnp
from jax import lax
from jax.experimental import pallas as pl
from jax.experimental.pallas import tpu as pltpu
from jax.sharding import PartitionSpec as P

HD = 128
ENC = 896
SPAN = 64
NB_LEN = 128
CHUNKS = 4
LEAD = 2


def shifted(array, axis, by):
    count = lax.axis_size(axis)
    pairs = [(i, i + by) for i in range(count) if 0 <= i + by < count]
    return lax.ppermute(array, axis, pairs)


def one_hot(index, count):
    return (index[:, None] == jnp.arange(count, dtype=jnp.int32)[None, :]).astype(jnp.int32)


def _row_sum_kernel(rows_ref, *refs):
    part_refs, out_ref = refs[:-1], refs[-1]
    block_rows = out_ref.shape[0]
    first = pl.program_id(0) * block_rows
    out_ref[...] = jnp.zeros(out_ref.shape, out_ref.dtype)
    base = 0
    for part in part_refs:

        def body(s, carry, part=part, base=base):
            local = rows_ref[base + s] - first

            @pl.when((local >= 0) & (local < block_rows))
            def _():
                out_ref[local] += part[s].astype(jnp.float32)

            return carry

        lax.fori_loop(0, part.shape[0], body, 0)
        base += part.shape[0]


def row_sums(rows, parts, row_count):
    width = parts[0].shape[1:]
    block_rows = 8 if row_count % 8 == 0 else row_count
    whole = lambda r, rows_ref: (0, 0, 0)
    return pl.pallas_call(
        _row_sum_kernel,
        grid_spec=pltpu.PrefetchScalarGridSpec(
            num_scalar_prefetch=1,
            grid=(row_count // block_rows,),
            in_specs=[pl.BlockSpec(p.shape, whole) for p in parts],
            out_specs=pl.BlockSpec((block_rows,) + width, lambda r, rows_ref: (r, 0, 0)),
        ),
        out_shape=jax.ShapeDtypeStruct((row_count,) + width, jnp.float32),
    )(rows, *parts)


def attend_chunk(query_blocks, grad_blocks, neighbours, key_weight, value_weight, head_count):
    block_count = query_blocks.shape[0]
    near_len = neighbours.shape[0] // block_count
    key_rows = jnp.dot(neighbours, key_weight, preferred_element_type=jnp.float32).astype(
        jnp.bfloat16
    )
    value_rows = jnp.dot(neighbours, value_weight, preferred_element_type=jnp.float32).astype(
        jnp.bfloat16
    )
    key_heads = key_rows.reshape(block_count, near_len, head_count, HD)
    value_heads = value_rows.reshape(block_count, near_len, head_count, HD)
    score_scale = HD ** (-0.5)
    scores = (
        jnp.einsum("cqhd,ckhd->chqk", query_blocks, key_heads, preferred_element_type=jnp.float32)
        * score_scale
    )
    weights = jnp.exp(scores)
    weights = weights / jnp.sum(weights, axis=-1, keepdims=True)
    weight_half = weights.astype(jnp.bfloat16)
    context_shift = jnp.einsum(
        "chqk,ckhd->cqhd", weight_half, value_heads, preferred_element_type=jnp.float32
    ).astype(jnp.bfloat16)
    prob_grads = jnp.einsum(
        "cqhd,ckhd->chqk", grad_blocks, value_heads, preferred_element_type=jnp.float32
    )
    row_delta = jnp.sum(weights * prob_grads, axis=-1, keepdims=True)
    score_grads = (score_scale * weights * (prob_grads - row_delta)).astype(jnp.bfloat16)
    query_shift = jnp.einsum(
        "chqk,ckhd->cqhd", score_grads, key_heads, preferred_element_type=jnp.float32
    ).astype(jnp.bfloat16)
    key_grads = jnp.einsum(
        "chqk,cqhd->ckhd", score_grads, query_blocks, preferred_element_type=jnp.float32
    ).astype(jnp.bfloat16)
    value_grads = jnp.einsum(
        "chqk,cqhd->ckhd", weight_half, grad_blocks, preferred_element_type=jnp.float32
    ).astype(jnp.bfloat16)
    feat_width = head_count * HD
    proj_grads = jnp.concatenate(
        [
            key_grads.reshape(block_count * near_len, feat_width),
            value_grads.reshape(block_count * near_len, feat_width),
        ],
        axis=1,
    )
    both_weights = jnp.concatenate([key_weight, value_weight], axis=1)
    near_grads = jnp.einsum(
        "pz,xz->px", proj_grads, both_weights, preferred_element_type=jnp.float32
    )
    return context_shift, query_shift, proj_grads, near_grads


def local(queries, d_context, database, key_weight, value_weight, neighbour_shard, neighbour_row):
    seq_count, seq_span, feat_width = queries.shape
    head_count = feat_width // HD
    lag_rows = SPAN - 1
    block_count = seq_count * seq_span // SPAN
    pick_count = neighbour_shard.shape[-1]
    ref_count = block_count * pick_count
    shard_count = lax.axis_size("dp")
    seq_total = lax.axis_size("seq")
    capacity = 2 * ref_count // shard_count
    chunk_count = CHUNKS if block_count % CHUNKS == 0 else 1
    chunk_blocks = block_count // chunk_count
    chunk_refs = chunk_blocks * pick_count
    chunk_cap = min(chunk_blocks, capacity)
    chunk_slots = shard_count * chunk_cap

    target = neighbour_shard.reshape(chunk_count, chunk_refs)
    wanted = neighbour_row.reshape(chunk_count, chunk_refs)
    slot_indices = []
    requests = []
    slot_refs = []
    for g in range(chunk_count):
        owners = one_hot(target[g], shard_count)
        before = jnp.cumsum(owners, axis=0) - owners
        slot_rank = jnp.sum(before * owners, axis=1)
        slot_index = target[g] * chunk_cap + slot_rank
        placed = one_hot(slot_index, chunk_slots)
        requests.append(
            jnp.sum(placed * wanted[g][:, None], axis=0).reshape(shard_count, 1, chunk_cap)
        )
        ref_ids = jnp.arange(1, chunk_refs + 1, dtype=jnp.int32)
        slot_refs.append(jnp.sum(placed * ref_ids[:, None], axis=0))
        slot_indices.append(slot_index)
    request = jnp.concatenate(requests, axis=1)
    arrived = lax.all_to_all(request, "dp", split_axis=0, concat_axis=0, tiled=True)

    head_rows, head_grads = shifted((queries[:, :lag_rows], d_context[:, :lag_rows]), "seq", -1)
    query_blocks = jnp.concatenate([queries[:, lag_rows:], head_rows], axis=1).reshape(
        block_count, SPAN, head_count, HD
    )
    grad_blocks = jnp.concatenate([d_context[:, lag_rows:], head_grads], axis=1).reshape(
        block_count, SPAN, head_count, HD
    )

    enc_share = ENC // (shard_count * seq_total)
    fetched = []
    link = None
    for g in range(chunk_count):
        rows = jnp.take(database, arrived[:, g, :].reshape(chunk_slots), axis=0)
        if link is not None:
            rows, _ = lax.optimization_barrier((rows, link))
        link = lax.all_to_all(rows, "dp", split_axis=0, concat_axis=0, tiled=True)
        fetched.append((rows, link))

    context_parts = []
    query_parts = []
    grads_out = []
    seq_major = []
    proj_parts = []

    def weight_term(first, last):
        return jnp.einsum(
            "px,pz->xz",
            jnp.concatenate(seq_major[first:last], axis=0),
            jnp.concatenate(proj_parts[first:last], axis=0),
            preferred_element_type=jnp.float32,
        )

    for g in range(chunk_count):
        incoming = fetched[g][1]
        if g + 1 < chunk_count:
            incoming, _ = lax.optimization_barrier((incoming, fetched[g + 1][0]))
        if g >= 1 and g == chunk_count - 1:
            early_terms = weight_term(0, g)
            incoming, early_terms = lax.optimization_barrier((incoming, early_terms))
        neighbours = jnp.take(incoming, slot_indices[g], axis=0).reshape(
            chunk_refs * NB_LEN, ENC
        )
        blocks = slice(g * chunk_blocks, (g + 1) * chunk_blocks)
        context_shift, query_shift, proj_grads, near_grads = attend_chunk(
            query_blocks[blocks], grad_blocks[blocks], neighbours, key_weight, value_weight,
            head_count,
        )
        context_parts.append(context_shift)
        query_parts.append(query_shift)
        padded = jnp.concatenate(
            [
                jnp.zeros((1, NB_LEN, ENC), jnp.bfloat16),
                near_grads.astype(jnp.bfloat16).reshape(chunk_refs, NB_LEN, ENC),
            ],
            axis=0,
        )
        grads_out.append(jnp.take(padded, slot_refs[g], axis=0))
        seq_major.append(
            neighbours.reshape(chunk_refs * NB_LEN, shard_count, seq_total, enc_share)
            .transpose(0, 2, 1, 3)
            .reshape(chunk_refs * NB_LEN, ENC)
        )
        proj_parts.append(proj_grads)

    weight_terms = weight_term(chunk_count - 1, chunk_count)
    if chunk_count > 1:
        weight_terms = early_terms + weight_terms

    plane_sums = lax.psum_scatter(
        weight_terms.reshape(seq_total, shard_count * enc_share, 2 * feat_width),
        "seq",
        scatter_dimension=0,
        tiled=True,
    )
    returned_parts = []
    for g in range(chunk_count):
        sent, _ = lax.optimization_barrier((grads_out[g], link))
        if g == chunk_count // 2:
            sent, plane_sums = lax.optimization_barrier((sent, plane_sums))
        link = lax.all_to_all(sent, "dp", split_axis=0, concat_axis=0, tiled=True)
        returned_parts.append(link)
    slot_rows = arrived.transpose(1, 0, 2).reshape(-1)
    database_grad = row_sums(slot_rows, returned_parts, database.shape[0])

    context_shift = jnp.concatenate(context_parts, axis=0).reshape(seq_count, seq_span, feat_width)
    query_shift = jnp.concatenate(query_parts, axis=0).reshape(seq_count, seq_span, feat_width)
    keep_rows = seq_span - lag_rows
    prior_context, prior_grads = shifted(
        (context_shift[:, keep_rows:], query_shift[:, keep_rows:]), "seq", 1
    )
    context = jnp.concatenate([prior_context, context_shift[:, :keep_rows]], axis=1)
    query_grad = jnp.concatenate([prior_grads, query_shift[:, :keep_rows]], axis=1)

    owned_grads = lax.psum_scatter(
        plane_sums.reshape(shard_count, enc_share, 2 * feat_width),
        "dp",
        scatter_dimension=0,
        tiled=True,
    ).reshape(enc_share, 2 * feat_width)
    return (
        context,
        query_grad,
        database_grad,
        owned_grads[:, :feat_width],
        owned_grads[:, feat_width:],
    )


def solution(mesh):
    return jax.shard_map(
        local,
        mesh=mesh,
        in_specs=(
            P("dp", "seq", None),
            P("dp", "seq", None),
            P(("dp", "seq"), None, None),
            P(),
            P(),
            P("dp", "seq", None, None),
            P("dp", "seq", None, None),
        ),
        out_specs=(
            P("dp", "seq", None),
            P("dp", "seq", None),
            P(("dp", "seq"), None, None),
            P(("dp", "seq"), None),
            P(("dp", "seq"), None),
        ),
        check_vma=False,
    )
```

```python
import jax
import jax.numpy as jnp
from jax import lax
from jax.experimental import pallas as pl
from jax.experimental.pallas import tpu as pltpu
from jax.sharding import PartitionSpec as P

HD = 128
ENC = 896
SPAN = 64
NB_LEN = 128
CHUNKS = 4
LEAD = 2


def shifted(array, axis, by):
    count = lax.axis_size(axis)
    pairs = [(i, i + by) for i in range(count) if 0 <= i + by < count]
    return lax.ppermute(array, axis, pairs)


def one_hot(index, count):
    return (index[:, None] == jnp.arange(count, dtype=jnp.int32)[None, :]).astype(jnp.int32)


def _row_sum_kernel(rows_ref, *refs):
    part_refs, out_ref = refs[:-1], refs[-1]
    block_rows = out_ref.shape[0]
    first = pl.program_id(0) * block_rows
    out_ref[...] = jnp.zeros(out_ref.shape, out_ref.dtype)
    base = 0
    for part in part_refs:

        def body(s, carry, part=part, base=base):
            local = rows_ref[base + s] - first

            @pl.when((local >= 0) & (local < block_rows))
            def _():
                out_ref[local] += part[s].astype(jnp.float32)

            return carry

        lax.fori_loop(0, part.shape[0], body, 0)
        base += part.shape[0]


def row_sums(rows, parts, row_count):
    width = parts[0].shape[1:]
    block_rows = 8 if row_count % 8 == 0 else row_count
    whole = lambda r, rows_ref: (0, 0, 0)
    return pl.pallas_call(
        _row_sum_kernel,
        grid_spec=pltpu.PrefetchScalarGridSpec(
            num_scalar_prefetch=1,
            grid=(row_count // block_rows,),
            in_specs=[pl.BlockSpec(p.shape, whole) for p in parts],
            out_specs=pl.BlockSpec((block_rows,) + width, lambda r, rows_ref: (r, 0, 0)),
        ),
        out_shape=jax.ShapeDtypeStruct((row_count,) + width, jnp.float32),
    )(rows, *parts)


def attend_chunk(query_blocks, grad_blocks, neighbours, key_weight, value_weight, head_count):
    block_count = query_blocks.shape[0]
    near_len = neighbours.shape[0] // block_count
    key_rows = jnp.dot(neighbours, key_weight, preferred_element_type=jnp.float32).astype(
        jnp.bfloat16
    )
    value_rows = jnp.dot(neighbours, value_weight, preferred_element_type=jnp.float32).astype(
        jnp.bfloat16
    )
    key_heads = key_rows.reshape(block_count, near_len, head_count, HD)
    value_heads = value_rows.reshape(block_count, near_len, head_count, HD)
    score_scale = HD ** (-0.5)
    scores = (
        jnp.einsum("cqhd,ckhd->chqk", query_blocks, key_heads, preferred_element_type=jnp.float32)
        * score_scale
    )
    weights = jnp.exp(scores)
    weights = weights / jnp.sum(weights, axis=-1, keepdims=True)
    weight_half = weights.astype(jnp.bfloat16)
    context_shift = jnp.einsum(
        "chqk,ckhd->cqhd", weight_half, value_heads, preferred_element_type=jnp.float32
    ).astype(jnp.bfloat16)
    prob_grads = jnp.einsum(
        "cqhd,ckhd->chqk", grad_blocks, value_heads, preferred_element_type=jnp.float32
    )
    row_delta = jnp.sum(weights * prob_grads, axis=-1, keepdims=True)
    score_grads = (score_scale * weights * (prob_grads - row_delta)).astype(jnp.bfloat16)
    query_shift = jnp.einsum(
        "chqk,ckhd->cqhd", score_grads, key_heads, preferred_element_type=jnp.float32
    ).astype(jnp.bfloat16)
    key_grads = jnp.einsum(
        "chqk,cqhd->ckhd", score_grads, query_blocks, preferred_element_type=jnp.float32
    ).astype(jnp.bfloat16)
    value_grads = jnp.einsum(
        "chqk,cqhd->ckhd", weight_half, grad_blocks, preferred_element_type=jnp.float32
    ).astype(jnp.bfloat16)
    feat_width = head_count * HD
    proj_grads = jnp.concatenate(
        [
            key_grads.reshape(block_count * near_len, feat_width),
            value_grads.reshape(block_count * near_len, feat_width),
        ],
        axis=1,
    )
    both_weights = jnp.concatenate([key_weight, value_weight], axis=1)
    near_grads = jnp.einsum(
        "pz,xz->px", proj_grads, both_weights, preferred_element_type=jnp.float32
    )
    return context_shift, query_shift, proj_grads, near_grads


def local(queries, d_context, database, key_weight, value_weight, neighbour_shard, neighbour_row):
    seq_count, seq_span, feat_width = queries.shape
    head_count = feat_width // HD
    lag_rows = SPAN - 1
    block_count = seq_count * seq_span // SPAN
    pick_count = neighbour_shard.shape[-1]
    ref_count = block_count * pick_count
    shard_count = lax.axis_size("dp")
    seq_total = lax.axis_size("seq")
    capacity = 2 * ref_count // shard_count
    chunk_count = CHUNKS if block_count % CHUNKS == 0 else 1
    chunk_blocks = block_count // chunk_count
    chunk_refs = chunk_blocks * pick_count
    chunk_cap = min(chunk_blocks, capacity)
    chunk_slots = shard_count * chunk_cap

    target = neighbour_shard.reshape(chunk_count, chunk_refs)
    wanted = neighbour_row.reshape(chunk_count, chunk_refs)
    slot_indices = []
    requests = []
    slot_refs = []
    for g in range(chunk_count):
        owners = one_hot(target[g], shard_count)
        before = jnp.cumsum(owners, axis=0) - owners
        slot_rank = jnp.sum(before * owners, axis=1)
        slot_index = target[g] * chunk_cap + slot_rank
        placed = one_hot(slot_index, chunk_slots)
        requests.append(
            jnp.sum(placed * wanted[g][:, None], axis=0).reshape(shard_count, 1, chunk_cap)
        )
        ref_ids = jnp.arange(1, chunk_refs + 1, dtype=jnp.int32)
        slot_refs.append(jnp.sum(placed * ref_ids[:, None], axis=0))
        slot_indices.append(slot_index)
    request = jnp.concatenate(requests, axis=1)
    arrived = lax.all_to_all(request, "dp", split_axis=0, concat_axis=0, tiled=True)

    head_rows, head_grads = shifted((queries[:, :lag_rows], d_context[:, :lag_rows]), "seq", -1)
    query_blocks = jnp.concatenate([queries[:, lag_rows:], head_rows], axis=1).reshape(
        block_count, SPAN, head_count, HD
    )
    grad_blocks = jnp.concatenate([d_context[:, lag_rows:], head_grads], axis=1).reshape(
        block_count, SPAN, head_count, HD
    )

    enc_share = ENC // (shard_count * seq_total)
    fetched = []
    link = None
    for g in range(chunk_count):
        rows = jnp.take(database, arrived[:, g, :].reshape(chunk_slots), axis=0)
        if link is not None:
            rows, _ = lax.optimization_barrier((rows, link))
        link = lax.all_to_all(rows, "dp", split_axis=0, concat_axis=0, tiled=True)
        fetched.append((rows, link))

    context_parts = []
    query_parts = []
    grads_out = []
    seq_major = []
    proj_parts = []
    for g in range(chunk_count):
        incoming = fetched[g][1]
        if g + 1 < chunk_count:
            incoming, _ = lax.optimization_barrier((incoming, fetched[g + 1][0]))
        neighbours = jnp.take(incoming, slot_indices[g], axis=0).reshape(
            chunk_refs * NB_LEN, ENC
        )
        blocks = slice(g * chunk_blocks, (g + 1) * chunk_blocks)
        context_shift, query_shift, proj_grads, near_grads = attend_chunk(
            query_blocks[blocks], grad_blocks[blocks], neighbours, key_weight, value_weight,
            head_count,
        )
        context_parts.append(context_shift)
        query_parts.append(query_shift)
        padded = jnp.concatenate(
            [
                jnp.zeros((1, NB_LEN, ENC), jnp.bfloat16),
                near_grads.astype(jnp.bfloat16).reshape(chunk_refs, NB_LEN, ENC),
            ],
            axis=0,
        )
        grads_out.append(jnp.take(padded, slot_refs[g], axis=0))
        seq_major.append(
            neighbours.reshape(chunk_refs * NB_LEN, shard_count, seq_total, enc_share)
            .transpose(0, 2, 1, 3)
            .reshape(chunk_refs * NB_LEN, ENC)
        )
        proj_parts.append(proj_grads)

    def weight_term(first, last):
        return jnp.einsum(
            "px,pz->xz",
            jnp.concatenate(seq_major[first:last], axis=0),
            jnp.concatenate(proj_parts[first:last], axis=0),
            preferred_element_type=jnp.float32,
        )

    first_sent, _ = lax.optimization_barrier((grads_out[0], link))
    proj_parts[-1], first_sent = lax.optimization_barrier((proj_parts[-1], first_sent))
    weight_terms = weight_term(chunk_count - 1, chunk_count)
    if chunk_count > 1:
        weight_terms = weight_term(0, chunk_count - 1) + weight_terms

    plane_sums = lax.psum_scatter(
        weight_terms.reshape(seq_total, shard_count * enc_share, 2 * feat_width),
        "seq",
        scatter_dimension=0,
        tiled=True,
    )
    returned_parts = []
    for g in range(chunk_count):
        if g == 0:
            sent = first_sent
        else:
            sent, _ = lax.optimization_barrier((grads_out[g], link))
        if g == chunk_count // 2:
            sent, plane_sums = lax.optimization_barrier((sent, plane_sums))
        link = lax.all_to_all(sent, "dp", split_axis=0, concat_axis=0, tiled=True)
        returned_parts.append(link)
    slot_rows = arrived.transpose(1, 0, 2).reshape(-1)
    database_grad = row_sums(slot_rows, returned_parts, database.shape[0])

    context_shift = jnp.concatenate(context_parts, axis=0).reshape(seq_count, seq_span, feat_width)
    query_shift = jnp.concatenate(query_parts, axis=0).reshape(seq_count, seq_span, feat_width)
    keep_rows = seq_span - lag_rows
    prior_context, prior_grads = shifted(
        (context_shift[:, keep_rows:], query_shift[:, keep_rows:]), "seq", 1
    )
    context = jnp.concatenate([prior_context, context_shift[:, :keep_rows]], axis=1)
    query_grad = jnp.concatenate([prior_grads, query_shift[:, :keep_rows]], axis=1)

    owned_grads = lax.psum_scatter(
        plane_sums.reshape(shard_count, enc_share, 2 * feat_width),
        "dp",
        scatter_dimension=0,
        tiled=True,
    ).reshape(enc_share, 2 * feat_width)
    return (
        context,
        query_grad,
        database_grad,
        owned_grads[:, :feat_width],
        owned_grads[:, feat_width:],
    )


def solution(mesh):
    return jax.shard_map(
        local,
        mesh=mesh,
        in_specs=(
            P("dp", "seq", None),
            P("dp", "seq", None),
            P(("dp", "seq"), None, None),
            P(),
            P(),
            P("dp", "seq", None, None),
            P("dp", "seq", None, None),
        ),
        out_specs=(
            P("dp", "seq", None),
            P("dp", "seq", None),
            P(("dp", "seq"), None, None),
            P(("dp", "seq"), None),
            P(("dp", "seq"), None),
        ),
        check_vma=False,
    )
```

```python
import jax
import jax.numpy as jnp
from jax import lax
from jax.experimental import pallas as pl
from jax.experimental.pallas import tpu as pltpu
from jax.sharding import PartitionSpec as P

HD = 128
ENC = 896
SPAN = 64
NB_LEN = 128
CHUNKS = 8
LEAD = 2


def shifted(array, axis, by):
    count = lax.axis_size(axis)
    pairs = [(i, i + by) for i in range(count) if 0 <= i + by < count]
    return lax.ppermute(array, axis, pairs)


def one_hot(index, count):
    return (index[:, None] == jnp.arange(count, dtype=jnp.int32)[None, :]).astype(jnp.int32)


def _row_sum_kernel(rows_ref, *refs):
    part_refs, out_ref = refs[:-1], refs[-1]
    block_rows = out_ref.shape[0]
    first = pl.program_id(0) * block_rows
    out_ref[...] = jnp.zeros(out_ref.shape, out_ref.dtype)
    base = 0
    for part in part_refs:

        def body(s, carry, part=part, base=base):
            local = rows_ref[base + s] - first

            @pl.when((local >= 0) & (local < block_rows))
            def _():
                out_ref[local] += part[s].astype(jnp.float32)

            return carry

        lax.fori_loop(0, part.shape[0], body, 0)
        base += part.shape[0]


def row_sums(rows, parts, row_count):
    width = parts[0].shape[1:]
    block_rows = 8 if row_count % 8 == 0 else row_count
    whole = lambda r, rows_ref: (0, 0, 0)
    return pl.pallas_call(
        _row_sum_kernel,
        grid_spec=pltpu.PrefetchScalarGridSpec(
            num_scalar_prefetch=1,
            grid=(row_count // block_rows,),
            in_specs=[pl.BlockSpec(p.shape, whole) for p in parts],
            out_specs=pl.BlockSpec((block_rows,) + width, lambda r, rows_ref: (r, 0, 0)),
        ),
        out_shape=jax.ShapeDtypeStruct((row_count,) + width, jnp.float32),
    )(rows, *parts)


def attend_chunk(query_blocks, grad_blocks, neighbours, key_weight, value_weight, head_count):
    block_count = query_blocks.shape[0]
    near_len = neighbours.shape[0] // block_count
    key_rows = jnp.dot(neighbours, key_weight, preferred_element_type=jnp.float32).astype(
        jnp.bfloat16
    )
    value_rows = jnp.dot(neighbours, value_weight, preferred_element_type=jnp.float32).astype(
        jnp.bfloat16
    )
    key_heads = key_rows.reshape(block_count, near_len, head_count, HD)
    value_heads = value_rows.reshape(block_count, near_len, head_count, HD)
    score_scale = HD ** (-0.5)
    scores = (
        jnp.einsum("cqhd,ckhd->chqk", query_blocks, key_heads, preferred_element_type=jnp.float32)
        * score_scale
    )
    weights = jnp.exp(scores)
    weights = weights / jnp.sum(weights, axis=-1, keepdims=True)
    weight_half = weights.astype(jnp.bfloat16)
    context_shift = jnp.einsum(
        "chqk,ckhd->cqhd", weight_half, value_heads, preferred_element_type=jnp.float32
    ).astype(jnp.bfloat16)
    prob_grads = jnp.einsum(
        "cqhd,ckhd->chqk", grad_blocks, value_heads, preferred_element_type=jnp.float32
    )
    row_delta = jnp.sum(weights * prob_grads, axis=-1, keepdims=True)
    score_grads = (score_scale * weights * (prob_grads - row_delta)).astype(jnp.bfloat16)
    query_shift = jnp.einsum(
        "chqk,ckhd->cqhd", score_grads, key_heads, preferred_element_type=jnp.float32
    ).astype(jnp.bfloat16)
    key_grads = jnp.einsum(
        "chqk,cqhd->ckhd", score_grads, query_blocks, preferred_element_type=jnp.float32
    ).astype(jnp.bfloat16)
    value_grads = jnp.einsum(
        "chqk,cqhd->ckhd", weight_half, grad_blocks, preferred_element_type=jnp.float32
    ).astype(jnp.bfloat16)
    feat_width = head_count * HD
    proj_grads = jnp.concatenate(
        [
            key_grads.reshape(block_count * near_len, feat_width),
            value_grads.reshape(block_count * near_len, feat_width),
        ],
        axis=1,
    )
    both_weights = jnp.concatenate([key_weight, value_weight], axis=1)
    near_grads = jnp.einsum(
        "pz,xz->px", proj_grads, both_weights, preferred_element_type=jnp.float32
    )
    return context_shift, query_shift, proj_grads, near_grads


def local(queries, d_context, database, key_weight, value_weight, neighbour_shard, neighbour_row):
    seq_count, seq_span, feat_width = queries.shape
    head_count = feat_width // HD
    lag_rows = SPAN - 1
    block_count = seq_count * seq_span // SPAN
    pick_count = neighbour_shard.shape[-1]
    ref_count = block_count * pick_count
    shard_count = lax.axis_size("dp")
    seq_total = lax.axis_size("seq")
    capacity = 2 * ref_count // shard_count
    chunk_count = CHUNKS if block_count % CHUNKS == 0 else 1
    chunk_blocks = block_count // chunk_count
    chunk_refs = chunk_blocks * pick_count
    chunk_cap = min(chunk_blocks, capacity)
    chunk_slots = shard_count * chunk_cap

    target = neighbour_shard.reshape(chunk_count, chunk_refs)
    wanted = neighbour_row.reshape(chunk_count, chunk_refs)
    slot_indices = []
    requests = []
    slot_refs = []
    for g in range(chunk_count):
        owners = one_hot(target[g], shard_count)
        before = jnp.cumsum(owners, axis=0) - owners
        slot_rank = jnp.sum(before * owners, axis=1)
        slot_index = target[g] * chunk_cap + slot_rank
        placed = one_hot(slot_index, chunk_slots)
        requests.append(
            jnp.sum(placed * wanted[g][:, None], axis=0).reshape(shard_count, 1, chunk_cap)
        )
        ref_ids = jnp.arange(1, chunk_refs + 1, dtype=jnp.int32)
        slot_refs.append(jnp.sum(placed * ref_ids[:, None], axis=0))
        slot_indices.append(slot_index)
    request = jnp.concatenate(requests, axis=1)
    arrived = lax.all_to_all(request, "dp", split_axis=0, concat_axis=0, tiled=True)

    head_rows, head_grads = shifted((queries[:, :lag_rows], d_context[:, :lag_rows]), "seq", -1)
    query_blocks = jnp.concatenate([queries[:, lag_rows:], head_rows], axis=1).reshape(
        block_count, SPAN, head_count, HD
    )
    grad_blocks = jnp.concatenate([d_context[:, lag_rows:], head_grads], axis=1).reshape(
        block_count, SPAN, head_count, HD
    )

    enc_share = ENC // (shard_count * seq_total)
    fetched = []
    link = None
    for g in range(chunk_count):
        rows = jnp.take(database, arrived[:, g, :].reshape(chunk_slots), axis=0)
        if link is not None:
            rows, _ = lax.optimization_barrier((rows, link))
        link = lax.all_to_all(rows, "dp", split_axis=0, concat_axis=0, tiled=True)
        fetched.append((rows, link))

    context_parts = []
    query_parts = []
    grads_out = []
    seq_major = []
    proj_parts = []
    for g in range(chunk_count):
        incoming = fetched[g][1]
        if g + 1 < chunk_count:
            incoming, _ = lax.optimization_barrier((incoming, fetched[g + 1][0]))
        neighbours = jnp.take(incoming, slot_indices[g], axis=0).reshape(
            chunk_refs * NB_LEN, ENC
        )
        blocks = slice(g * chunk_blocks, (g + 1) * chunk_blocks)
        context_shift, query_shift, proj_grads, near_grads = attend_chunk(
            query_blocks[blocks], grad_blocks[blocks], neighbours, key_weight, value_weight,
            head_count,
        )
        context_parts.append(context_shift)
        query_parts.append(query_shift)
        padded = jnp.concatenate(
            [
                jnp.zeros((1, NB_LEN, ENC), jnp.bfloat16),
                near_grads.astype(jnp.bfloat16).reshape(chunk_refs, NB_LEN, ENC),
            ],
            axis=0,
        )
        grads_out.append(jnp.take(padded, slot_refs[g], axis=0))
        seq_major.append(
            neighbours.reshape(chunk_refs * NB_LEN, shard_count, seq_total, enc_share)
            .transpose(0, 2, 1, 3)
            .reshape(chunk_refs * NB_LEN, ENC)
        )
        proj_parts.append(proj_grads)

    def weight_term(first, last):
        return jnp.einsum(
            "px,pz->xz",
            jnp.concatenate(seq_major[first:last], axis=0),
            jnp.concatenate(proj_parts[first:last], axis=0),
            preferred_element_type=jnp.float32,
        )

    weight_terms = weight_term(chunk_count - 1, chunk_count)
    if chunk_count > 1:
        weight_terms = weight_term(0, chunk_count - 1) + weight_terms

    plane_sums = lax.psum_scatter(
        weight_terms.reshape(seq_total, shard_count * enc_share, 2 * feat_width),
        "seq",
        scatter_dimension=0,
        tiled=True,
    )
    returned_parts = []
    for g in range(chunk_count):
        sent, _ = lax.optimization_barrier((grads_out[g], link))
        if g == chunk_count // 2:
            sent, plane_sums = lax.optimization_barrier((sent, plane_sums))
        link = lax.all_to_all(sent, "dp", split_axis=0, concat_axis=0, tiled=True)
        returned_parts.append(link)
    slot_rows = arrived.transpose(1, 0, 2).reshape(-1)
    database_grad = row_sums(slot_rows, returned_parts, database.shape[0])

    context_shift = jnp.concatenate(context_parts, axis=0).reshape(seq_count, seq_span, feat_width)
    query_shift = jnp.concatenate(query_parts, axis=0).reshape(seq_count, seq_span, feat_width)
    keep_rows = seq_span - lag_rows
    prior_context, prior_grads = shifted(
        (context_shift[:, keep_rows:], query_shift[:, keep_rows:]), "seq", 1
    )
    context = jnp.concatenate([prior_context, context_shift[:, :keep_rows]], axis=1)
    query_grad = jnp.concatenate([prior_grads, query_shift[:, :keep_rows]], axis=1)

    owned_grads = lax.psum_scatter(
        plane_sums.reshape(shard_count, enc_share, 2 * feat_width),
        "dp",
        scatter_dimension=0,
        tiled=True,
    ).reshape(enc_share, 2 * feat_width)
    return (
        context,
        query_grad,
        database_grad,
        owned_grads[:, :feat_width],
        owned_grads[:, feat_width:],
    )


def solution(mesh):
    return jax.shard_map(
        local,
        mesh=mesh,
        in_specs=(
            P("dp", "seq", None),
            P("dp", "seq", None),
            P(("dp", "seq"), None, None),
            P(),
            P(),
            P("dp", "seq", None, None),
            P("dp", "seq", None, None),
        ),
        out_specs=(
            P("dp", "seq", None),
            P("dp", "seq", None),
            P(("dp", "seq"), None, None),
            P(("dp", "seq"), None),
            P(("dp", "seq"), None),
        ),
        check_vma=False,
    )
```

```python
import jax
import jax.numpy as jnp
from jax import lax
from jax.experimental import pallas as pl
from jax.experimental.pallas import tpu as pltpu
from jax.sharding import PartitionSpec as P

HD = 128
ENC = 896
SPAN = 64
NB_LEN = 128
CHUNKS = 2
LEAD = 2


def shifted(array, axis, by):
    count = lax.axis_size(axis)
    pairs = [(i, i + by) for i in range(count) if 0 <= i + by < count]
    return lax.ppermute(array, axis, pairs)


def one_hot(index, count):
    return (index[:, None] == jnp.arange(count, dtype=jnp.int32)[None, :]).astype(jnp.int32)


def _row_sum_kernel(rows_ref, *refs):
    part_refs, out_ref = refs[:-1], refs[-1]
    block_rows = out_ref.shape[0]
    first = pl.program_id(0) * block_rows
    out_ref[...] = jnp.zeros(out_ref.shape, out_ref.dtype)
    base = 0
    for part in part_refs:

        def body(s, carry, part=part, base=base):
            local = rows_ref[base + s] - first

            @pl.when((local >= 0) & (local < block_rows))
            def _():
                out_ref[local] += part[s].astype(jnp.float32)

            return carry

        lax.fori_loop(0, part.shape[0], body, 0)
        base += part.shape[0]


def row_sums(rows, parts, row_count):
    width = parts[0].shape[1:]
    block_rows = 8 if row_count % 8 == 0 else row_count
    whole = lambda r, rows_ref: (0, 0, 0)
    return pl.pallas_call(
        _row_sum_kernel,
        grid_spec=pltpu.PrefetchScalarGridSpec(
            num_scalar_prefetch=1,
            grid=(row_count // block_rows,),
            in_specs=[pl.BlockSpec(p.shape, whole) for p in parts],
            out_specs=pl.BlockSpec((block_rows,) + width, lambda r, rows_ref: (r, 0, 0)),
        ),
        out_shape=jax.ShapeDtypeStruct((row_count,) + width, jnp.float32),
    )(rows, *parts)


def attend_chunk(query_blocks, grad_blocks, neighbours, key_weight, value_weight, head_count):
    block_count = query_blocks.shape[0]
    near_len = neighbours.shape[0] // block_count
    key_rows = jnp.dot(neighbours, key_weight, preferred_element_type=jnp.float32).astype(
        jnp.bfloat16
    )
    value_rows = jnp.dot(neighbours, value_weight, preferred_element_type=jnp.float32).astype(
        jnp.bfloat16
    )
    key_heads = key_rows.reshape(block_count, near_len, head_count, HD)
    value_heads = value_rows.reshape(block_count, near_len, head_count, HD)
    score_scale = HD ** (-0.5)
    scores = (
        jnp.einsum("cqhd,ckhd->chqk", query_blocks, key_heads, preferred_element_type=jnp.float32)
        * score_scale
    )
    weights = jnp.exp(scores)
    weights = weights / jnp.sum(weights, axis=-1, keepdims=True)
    weight_half = weights.astype(jnp.bfloat16)
    context_shift = jnp.einsum(
        "chqk,ckhd->cqhd", weight_half, value_heads, preferred_element_type=jnp.float32
    ).astype(jnp.bfloat16)
    prob_grads = jnp.einsum(
        "cqhd,ckhd->chqk", grad_blocks, value_heads, preferred_element_type=jnp.float32
    )
    row_delta = jnp.sum(weights * prob_grads, axis=-1, keepdims=True)
    score_grads = (score_scale * weights * (prob_grads - row_delta)).astype(jnp.bfloat16)
    query_shift = jnp.einsum(
        "chqk,ckhd->cqhd", score_grads, key_heads, preferred_element_type=jnp.float32
    ).astype(jnp.bfloat16)
    key_grads = jnp.einsum(
        "chqk,cqhd->ckhd", score_grads, query_blocks, preferred_element_type=jnp.float32
    ).astype(jnp.bfloat16)
    value_grads = jnp.einsum(
        "chqk,cqhd->ckhd", weight_half, grad_blocks, preferred_element_type=jnp.float32
    ).astype(jnp.bfloat16)
    feat_width = head_count * HD
    proj_grads = jnp.concatenate(
        [
            key_grads.reshape(block_count * near_len, feat_width),
            value_grads.reshape(block_count * near_len, feat_width),
        ],
        axis=1,
    )
    both_weights = jnp.concatenate([key_weight, value_weight], axis=1)
    near_grads = jnp.einsum(
        "pz,xz->px", proj_grads, both_weights, preferred_element_type=jnp.float32
    )
    return context_shift, query_shift, proj_grads, near_grads


def local(queries, d_context, database, key_weight, value_weight, neighbour_shard, neighbour_row):
    seq_count, seq_span, feat_width = queries.shape
    head_count = feat_width // HD
    lag_rows = SPAN - 1
    block_count = seq_count * seq_span // SPAN
    pick_count = neighbour_shard.shape[-1]
    ref_count = block_count * pick_count
    shard_count = lax.axis_size("dp")
    seq_total = lax.axis_size("seq")
    capacity = 2 * ref_count // shard_count
    chunk_count = CHUNKS if block_count % CHUNKS == 0 else 1
    chunk_blocks = block_count // chunk_count
    chunk_refs = chunk_blocks * pick_count
    chunk_cap = min(chunk_blocks, capacity)
    chunk_slots = shard_count * chunk_cap

    target = neighbour_shard.reshape(chunk_count, chunk_refs)
    wanted = neighbour_row.reshape(chunk_count, chunk_refs)
    slot_indices = []
    requests = []
    slot_refs = []
    for g in range(chunk_count):
        owners = one_hot(target[g], shard_count)
        before = jnp.cumsum(owners, axis=0) - owners
        slot_rank = jnp.sum(before * owners, axis=1)
        slot_index = target[g] * chunk_cap + slot_rank
        placed = one_hot(slot_index, chunk_slots)
        requests.append(
            jnp.sum(placed * wanted[g][:, None], axis=0).reshape(shard_count, 1, chunk_cap)
        )
        ref_ids = jnp.arange(1, chunk_refs + 1, dtype=jnp.int32)
        slot_refs.append(jnp.sum(placed * ref_ids[:, None], axis=0))
        slot_indices.append(slot_index)
    request = jnp.concatenate(requests, axis=1)
    arrived = lax.all_to_all(request, "dp", split_axis=0, concat_axis=0, tiled=True)

    head_rows, head_grads = shifted((queries[:, :lag_rows], d_context[:, :lag_rows]), "seq", -1)
    query_blocks = jnp.concatenate([queries[:, lag_rows:], head_rows], axis=1).reshape(
        block_count, SPAN, head_count, HD
    )
    grad_blocks = jnp.concatenate([d_context[:, lag_rows:], head_grads], axis=1).reshape(
        block_count, SPAN, head_count, HD
    )

    enc_share = ENC // (shard_count * seq_total)
    fetched = []
    link = None
    for g in range(chunk_count):
        rows = jnp.take(database, arrived[:, g, :].reshape(chunk_slots), axis=0)
        if link is not None:
            rows, _ = lax.optimization_barrier((rows, link))
        link = lax.all_to_all(rows, "dp", split_axis=0, concat_axis=0, tiled=True)
        fetched.append((rows, link))

    context_parts = []
    query_parts = []
    grads_out = []
    seq_major = []
    proj_parts = []
    for g in range(chunk_count):
        incoming = fetched[g][1]
        if g + 1 < chunk_count:
            incoming, _ = lax.optimization_barrier((incoming, fetched[g + 1][0]))
        neighbours = jnp.take(incoming, slot_indices[g], axis=0).reshape(
            chunk_refs * NB_LEN, ENC
        )
        blocks = slice(g * chunk_blocks, (g + 1) * chunk_blocks)
        context_shift, query_shift, proj_grads, near_grads = attend_chunk(
            query_blocks[blocks], grad_blocks[blocks], neighbours, key_weight, value_weight,
            head_count,
        )
        context_parts.append(context_shift)
        query_parts.append(query_shift)
        padded = jnp.concatenate(
            [
                jnp.zeros((1, NB_LEN, ENC), jnp.bfloat16),
                near_grads.astype(jnp.bfloat16).reshape(chunk_refs, NB_LEN, ENC),
            ],
            axis=0,
        )
        grads_out.append(jnp.take(padded, slot_refs[g], axis=0))
        seq_major.append(
            neighbours.reshape(chunk_refs * NB_LEN, shard_count, seq_total, enc_share)
            .transpose(0, 2, 1, 3)
            .reshape(chunk_refs * NB_LEN, ENC)
        )
        proj_parts.append(proj_grads)

    def weight_term(first, last):
        return jnp.einsum(
            "px,pz->xz",
            jnp.concatenate(seq_major[first:last], axis=0),
            jnp.concatenate(proj_parts[first:last], axis=0),
            preferred_element_type=jnp.float32,
        )

    weight_terms = weight_term(chunk_count - 1, chunk_count)
    if chunk_count > 1:
        weight_terms = weight_term(0, chunk_count - 1) + weight_terms

    plane_sums = lax.psum_scatter(
        weight_terms.reshape(seq_total, shard_count * enc_share, 2 * feat_width),
        "seq",
        scatter_dimension=0,
        tiled=True,
    )
    returned_parts = []
    for g in range(chunk_count):
        sent, _ = lax.optimization_barrier((grads_out[g], link))
        if g == chunk_count // 2:
            sent, plane_sums = lax.optimization_barrier((sent, plane_sums))
        link = lax.all_to_all(sent, "dp", split_axis=0, concat_axis=0, tiled=True)
        returned_parts.append(link)
    slot_rows = arrived.transpose(1, 0, 2).reshape(-1)
    database_grad = row_sums(slot_rows, returned_parts, database.shape[0])

    context_shift = jnp.concatenate(context_parts, axis=0).reshape(seq_count, seq_span, feat_width)
    query_shift = jnp.concatenate(query_parts, axis=0).reshape(seq_count, seq_span, feat_width)
    keep_rows = seq_span - lag_rows
    prior_context, prior_grads = shifted(
        (context_shift[:, keep_rows:], query_shift[:, keep_rows:]), "seq", 1
    )
    context = jnp.concatenate([prior_context, context_shift[:, :keep_rows]], axis=1)
    query_grad = jnp.concatenate([prior_grads, query_shift[:, :keep_rows]], axis=1)

    owned_grads = lax.psum_scatter(
        plane_sums.reshape(shard_count, enc_share, 2 * feat_width),
        "dp",
        scatter_dimension=0,
        tiled=True,
    ).reshape(enc_share, 2 * feat_width)
    return (
        context,
        query_grad,
        database_grad,
        owned_grads[:, :feat_width],
        owned_grads[:, feat_width:],
    )


def solution(mesh):
    return jax.shard_map(
        local,
        mesh=mesh,
        in_specs=(
            P("dp", "seq", None),
            P("dp", "seq", None),
            P(("dp", "seq"), None, None),
            P(),
            P(),
            P("dp", "seq", None, None),
            P("dp", "seq", None, None),
        ),
        out_specs=(
            P("dp", "seq", None),
            P("dp", "seq", None),
            P(("dp", "seq"), None, None),
            P(("dp", "seq"), None),
            P(("dp", "seq"), None),
        ),
        check_vma=False,
    )
```

```python
import jax
import jax.numpy as jnp
from jax import lax
from jax.experimental import pallas as pl
from jax.experimental.pallas import tpu as pltpu
from jax.sharding import PartitionSpec as P

HD = 128
ENC = 896
SPAN = 64
NB_LEN = 128
CHUNKS = 4
LEAD = 2


def shifted(array, axis, by):
    count = lax.axis_size(axis)
    pairs = [(i, i + by) for i in range(count) if 0 <= i + by < count]
    return lax.ppermute(array, axis, pairs)


def one_hot(index, count):
    return (index[:, None] == jnp.arange(count, dtype=jnp.int32)[None, :]).astype(jnp.int32)


def _row_sum_kernel(rows_ref, *refs):
    part_refs, out_ref = refs[:-1], refs[-1]
    block_rows = out_ref.shape[0]
    first = pl.program_id(0) * block_rows
    out_ref[...] = jnp.zeros(out_ref.shape, out_ref.dtype)
    base = 0
    for part in part_refs:

        def body(s, carry, part=part, base=base):
            local = rows_ref[base + s] - first

            @pl.when((local >= 0) & (local < block_rows))
            def _():
                out_ref[local] += part[s].astype(jnp.float32)

            return carry

        lax.fori_loop(0, part.shape[0], body, 0)
        base += part.shape[0]


def row_sums(rows, parts, row_count):
    width = parts[0].shape[1:]
    block_rows = 4 if row_count % 4 == 0 else row_count
    whole = lambda r, rows_ref: (0, 0, 0)
    return pl.pallas_call(
        _row_sum_kernel,
        grid_spec=pltpu.PrefetchScalarGridSpec(
            num_scalar_prefetch=1,
            grid=(row_count // block_rows,),
            in_specs=[pl.BlockSpec(p.shape, whole) for p in parts],
            out_specs=pl.BlockSpec((block_rows,) + width, lambda r, rows_ref: (r, 0, 0)),
        ),
        out_shape=jax.ShapeDtypeStruct((row_count,) + width, jnp.float32),
    )(rows, *parts)


def attend_chunk(query_blocks, grad_blocks, neighbours, key_weight, value_weight, head_count):
    block_count = query_blocks.shape[0]
    near_len = neighbours.shape[0] // block_count
    key_rows = jnp.dot(neighbours, key_weight, preferred_element_type=jnp.float32).astype(
        jnp.bfloat16
    )
    value_rows = jnp.dot(neighbours, value_weight, preferred_element_type=jnp.float32).astype(
        jnp.bfloat16
    )
    key_heads = key_rows.reshape(block_count, near_len, head_count, HD)
    value_heads = value_rows.reshape(block_count, near_len, head_count, HD)
    score_scale = HD ** (-0.5)
    scores = (
        jnp.einsum("cqhd,ckhd->chqk", query_blocks, key_heads, preferred_element_type=jnp.float32)
        * score_scale
    )
    weights = jnp.exp(scores)
    weights = weights / jnp.sum(weights, axis=-1, keepdims=True)
    weight_half = weights.astype(jnp.bfloat16)
    context_shift = jnp.einsum(
        "chqk,ckhd->cqhd", weight_half, value_heads, preferred_element_type=jnp.float32
    ).astype(jnp.bfloat16)
    prob_grads = jnp.einsum(
        "cqhd,ckhd->chqk", grad_blocks, value_heads, preferred_element_type=jnp.float32
    )
    row_delta = jnp.sum(weights * prob_grads, axis=-1, keepdims=True)
    score_grads = (score_scale * weights * (prob_grads - row_delta)).astype(jnp.bfloat16)
    query_shift = jnp.einsum(
        "chqk,ckhd->cqhd", score_grads, key_heads, preferred_element_type=jnp.float32
    ).astype(jnp.bfloat16)
    key_grads = jnp.einsum(
        "chqk,cqhd->ckhd", score_grads, query_blocks, preferred_element_type=jnp.float32
    ).astype(jnp.bfloat16)
    value_grads = jnp.einsum(
        "chqk,cqhd->ckhd", weight_half, grad_blocks, preferred_element_type=jnp.float32
    ).astype(jnp.bfloat16)
    feat_width = head_count * HD
    proj_grads = jnp.concatenate(
        [
            key_grads.reshape(block_count * near_len, feat_width),
            value_grads.reshape(block_count * near_len, feat_width),
        ],
        axis=1,
    )
    both_weights = jnp.concatenate([key_weight, value_weight], axis=1)
    near_grads = jnp.einsum(
        "pz,xz->px", proj_grads, both_weights, preferred_element_type=jnp.float32
    )
    return context_shift, query_shift, proj_grads, near_grads


def local(queries, d_context, database, key_weight, value_weight, neighbour_shard, neighbour_row):
    seq_count, seq_span, feat_width = queries.shape
    head_count = feat_width // HD
    lag_rows = SPAN - 1
    block_count = seq_count * seq_span // SPAN
    pick_count = neighbour_shard.shape[-1]
    ref_count = block_count * pick_count
    shard_count = lax.axis_size("dp")
    seq_total = lax.axis_size("seq")
    capacity = 2 * ref_count // shard_count
    chunk_count = CHUNKS if block_count % CHUNKS == 0 else 1
    chunk_blocks = block_count // chunk_count
    chunk_refs = chunk_blocks * pick_count
    chunk_cap = min(chunk_blocks, capacity)
    chunk_slots = shard_count * chunk_cap

    target = neighbour_shard.reshape(chunk_count, chunk_refs)
    wanted = neighbour_row.reshape(chunk_count, chunk_refs)
    slot_indices = []
    requests = []
    slot_refs = []
    for g in range(chunk_count):
        owners = one_hot(target[g], shard_count)
        before = jnp.cumsum(owners, axis=0) - owners
        slot_rank = jnp.sum(before * owners, axis=1)
        slot_index = target[g] * chunk_cap + slot_rank
        placed = one_hot(slot_index, chunk_slots)
        requests.append(
            jnp.sum(placed * wanted[g][:, None], axis=0).reshape(shard_count, 1, chunk_cap)
        )
        ref_ids = jnp.arange(1, chunk_refs + 1, dtype=jnp.int32)
        slot_refs.append(jnp.sum(placed * ref_ids[:, None], axis=0))
        slot_indices.append(slot_index)
    request = jnp.concatenate(requests, axis=1)
    arrived = lax.all_to_all(request, "dp", split_axis=0, concat_axis=0, tiled=True)

    head_rows, head_grads = shifted((queries[:, :lag_rows], d_context[:, :lag_rows]), "seq", -1)
    query_blocks = jnp.concatenate([queries[:, lag_rows:], head_rows], axis=1).reshape(
        block_count, SPAN, head_count, HD
    )
    grad_blocks = jnp.concatenate([d_context[:, lag_rows:], head_grads], axis=1).reshape(
        block_count, SPAN, head_count, HD
    )

    enc_share = ENC // (shard_count * seq_total)
    fetched = []
    link = None
    for g in range(chunk_count):
        rows = jnp.take(database, arrived[:, g, :].reshape(chunk_slots), axis=0)
        if link is not None:
            rows, _ = lax.optimization_barrier((rows, link))
        link = lax.all_to_all(rows, "dp", split_axis=0, concat_axis=0, tiled=True)
        fetched.append((rows, link))

    context_parts = []
    query_parts = []
    grads_out = []
    seq_major = []
    proj_parts = []
    for g in range(chunk_count):
        incoming = fetched[g][1]
        if g + 1 < chunk_count:
            incoming, _ = lax.optimization_barrier((incoming, fetched[g + 1][0]))
        neighbours = jnp.take(incoming, slot_indices[g], axis=0).reshape(
            chunk_refs * NB_LEN, ENC
        )
        blocks = slice(g * chunk_blocks, (g + 1) * chunk_blocks)
        context_shift, query_shift, proj_grads, near_grads = attend_chunk(
            query_blocks[blocks], grad_blocks[blocks], neighbours, key_weight, value_weight,
            head_count,
        )
        context_parts.append(context_shift)
        query_parts.append(query_shift)
        padded = jnp.concatenate(
            [
                jnp.zeros((1, NB_LEN, ENC), jnp.bfloat16),
                near_grads.astype(jnp.bfloat16).reshape(chunk_refs, NB_LEN, ENC),
            ],
            axis=0,
        )
        grads_out.append(jnp.take(padded, slot_refs[g], axis=0))
        seq_major.append(
            neighbours.reshape(chunk_refs * NB_LEN, shard_count, seq_total, enc_share)
            .transpose(0, 2, 1, 3)
            .reshape(chunk_refs * NB_LEN, ENC)
        )
        proj_parts.append(proj_grads)

    def weight_term(first, last):
        return jnp.einsum(
            "px,pz->xz",
            jnp.concatenate(seq_major[first:last], axis=0),
            jnp.concatenate(proj_parts[first:last], axis=0),
            preferred_element_type=jnp.float32,
        )

    weight_terms = weight_term(chunk_count - 1, chunk_count)
    if chunk_count > 1:
        weight_terms = weight_term(0, chunk_count - 1) + weight_terms

    plane_sums = lax.psum_scatter(
        weight_terms.reshape(seq_total, shard_count * enc_share, 2 * feat_width),
        "seq",
        scatter_dimension=0,
        tiled=True,
    )
    returned_parts = []
    for g in range(chunk_count):
        sent, _ = lax.optimization_barrier((grads_out[g], link))
        if g == chunk_count // 2:
            sent, plane_sums = lax.optimization_barrier((sent, plane_sums))
        link = lax.all_to_all(sent, "dp", split_axis=0, concat_axis=0, tiled=True)
        returned_parts.append(link)
    slot_rows = arrived.transpose(1, 0, 2).reshape(-1)
    database_grad = row_sums(slot_rows, returned_parts, database.shape[0])

    context_shift = jnp.concatenate(context_parts, axis=0).reshape(seq_count, seq_span, feat_width)
    query_shift = jnp.concatenate(query_parts, axis=0).reshape(seq_count, seq_span, feat_width)
    keep_rows = seq_span - lag_rows
    prior_context, prior_grads = shifted(
        (context_shift[:, keep_rows:], query_shift[:, keep_rows:]), "seq", 1
    )
    context = jnp.concatenate([prior_context, context_shift[:, :keep_rows]], axis=1)
    query_grad = jnp.concatenate([prior_grads, query_shift[:, :keep_rows]], axis=1)

    owned_grads = lax.psum_scatter(
        plane_sums.reshape(shard_count, enc_share, 2 * feat_width),
        "dp",
        scatter_dimension=0,
        tiled=True,
    ).reshape(enc_share, 2 * feat_width)
    return (
        context,
        query_grad,
        database_grad,
        owned_grads[:, :feat_width],
        owned_grads[:, feat_width:],
    )


def solution(mesh):
    return jax.shard_map(
        local,
        mesh=mesh,
        in_specs=(
            P("dp", "seq", None),
            P("dp", "seq", None),
            P(("dp", "seq"), None, None),
            P(),
            P(),
            P("dp", "seq", None, None),
            P("dp", "seq", None, None),
        ),
        out_specs=(
            P("dp", "seq", None),
            P("dp", "seq", None),
            P(("dp", "seq"), None, None),
            P(("dp", "seq"), None),
            P(("dp", "seq"), None),
        ),
        check_vma=False,
    )
```
